512 devices in a mesh: ctx: 64 (over x, y, core), fsdp: 8 (over z).
Axes of the slice: x: 4, y: 8, z: 8, core: 2. Of those that a mesh axis runs over, the one named last changes fastest.
Arguments:
- outer_gate: bfloat16 [2048, 16384], P('fsdp', 'ctx'), may hold values from -6 to 6
- inner_gate: bfloat16 [2048, 16384], P('fsdp', 'ctx'), may hold values from -6 to 6
- value_stream: bfloat16 [2048, 16384], P('fsdp', 'ctx'), may hold values from -6 to 6
- grad_output: bfloat16 [2048, 16384], P('fsdp', 'ctx'), may hold values from -6 to 6
- filters: float32 [128, 128], P('fsdp', 'ctx'), may hold values from -0.5 to 0.5
- feature_taps: float32 [3, 3, 2048], P(None, None, ('ctx', 'fsdp')), may hold values from -3 to 3
- skip_gain: float32 [2048], P(('ctx', 'fsdp')), may hold values from -4 to 4
Outputs:
- gated_out: bfloat16 [2048, 16384], P('fsdp', 'ctx')
- grad_outer: bfloat16 [2048, 16384], P('fsdp', 'ctx')
- grad_inner: bfloat16 [2048, 16384], P('fsdp', 'ctx')
- grad_value: bfloat16 [2048, 16384], P('fsdp', 'ctx')
- grad_filters: float32 [128, 128], P('fsdp', 'ctx')
- grad_taps: float32 [3, 3, 2048], P(None, None, ('ctx', 'fsdp'))
- grad_skip: float32 [2048], P(('ctx', 'fsdp'))
The draws below stay inside these ranges and needn't reach their ends.
All inputs are finite; a program needn't handle non-finite values.
Results may differ from the reference program's by a relative error of at most 0.03.
Values may be sent and summed in bfloat16 or wider, within the bound.
No kernel may reach another device: no remote copies, remote signals or barrier semaphores. Data moves between devices by JAX's collectives and lax.ppermute only.
A program may use at most 64 MiB of HBM per device.

```python
import math
import jax
import jax.numpy as jnp
from jax import lax

CH = 2048
GROUP_SIZE = 16
FILT = 128
TOK_DEV = 256
GROUPS = 128
LENGTH = 16384


def block_scale(own_key, dims, shards, least, top_value):
    factor_of = 1.0
    for axis_at, blocks in shards:
        steps = jax.random.uniform(jax.random.fold_in(jax.random.fold_in(own_key, 6), axis_at), (blocks,), jnp.float32, least / len(shards), top_value / len(shards))
        factor_of = factor_of * jnp.repeat(jnp.exp(steps), dims[axis_at] // blocks).reshape((-1,) + (1,) * (len(dims) - 1 - axis_at))
    return factor_of


def scatter_about(key, dims, scale, bound, cuts=(), kind=jnp.bfloat16):
    values = jax.random.normal(key, dims, jnp.float32) * scale
    if len(cuts) > 0:
        values = block_scale(key, dims, cuts, -0.22, 0.18) * values
    return jnp.clip(values, min=-bound, max=bound).astype(kind)


def setup_inputs(seed: int = 0) -> dict:
    splits = jax.random.split(jax.random.key(seed), 8)
    outer_gate = scatter_about(splits[0], (CH, LENGTH), 1.0, 6.0, ((0, 8), (1, 64)))
    inner_gate = scatter_about(splits[1], (CH, LENGTH), 1.0, 6.0, ((0, 8), (1, 64)))
    value_stream = scatter_about(splits[2], (CH, LENGTH), 1.0, 6.0, ((0, 8), (1, 64)))
    grad_output = scatter_about(splits[3], (CH, LENGTH), 1.0, 6.0, ((0, 8), (1, 64)))
    filters = scatter_about(splits[4], (GROUPS, FILT), FILT ** -0.5, 0.5, ((0, 8), (1, 64)), jnp.float32)
    feature_taps = scatter_about(splits[5], (3, 3, CH), 0.6, 3.0, ((2, 512),), jnp.float32)
    skip_gain = scatter_about(splits[6], (CH,), 1.0, 4.0, ((0, 512),), jnp.float32)
    return {"outer_gate": outer_gate, "inner_gate": inner_gate, "value_stream": value_stream, "grad_output": grad_output, "filters": filters, "feature_taps": feature_taps, "skip_gain": skip_gain}


def shifted_right(values, shift_by):
    return jnp.pad(values, ((0, 0), (shift_by, 0)))[:, :values.shape[1]]

def shifted_left(values, shift_by):
    return jnp.pad(values, ((0, 0), (0, shift_by)))[:, shift_by:]

def featurize(stream, tap_gains):
    stream_f = stream.astype(jnp.float32)
    result = tap_gains[0][:, None] * stream_f
    result = result + tap_gains[1][:, None] * shifted_right(stream_f, 1)
    return result + tap_gains[2][:, None] * shifted_right(stream_f, 2)

def carry_back(grad_rows, tap_gains):
    grad_f = grad_rows.astype(jnp.float32)
    result = tap_gains[0][:, None] * grad_f
    result = result + tap_gains[1][:, None] * shifted_left(grad_f, 1)
    return result + tap_gains[2][:, None] * shifted_left(grad_f, 2)

def tap_sums(grad_rows, stream):
    grad_f = grad_rows.astype(jnp.float32)
    stream_f = stream.astype(jnp.float32)
    return jnp.stack([lax.optimization_barrier(jnp.sum(grad_f * shifted_right(stream_f, shift_by), axis=1)) for shift_by in range(3)])

def toeplitz_rows(filters_low, block_len):
    groups, taps_count = filters_low.shape
    window = block_len + taps_count - 1
    filter_row = jnp.concatenate([filters_low[:, ::-1], jnp.zeros((groups, window + 1 - taps_count), filters_low.dtype)], axis=1)
    flattened = jnp.tile(filter_row, (1, block_len))[:, :block_len * window]
    return flattened.reshape(groups, block_len, window)

def skew_sum(cross_terms, taps_count):
    groups, block_len, window = cross_terms.shape
    flattened = jnp.pad(cross_terms.reshape(groups, block_len * window), ((0, 0), (0, block_len)))
    return lax.optimization_barrier(jnp.sum(flattened.reshape(groups, block_len, window + 1)[:, :, :taps_count], axis=1))[:, ::-1]

def causal_conv(values_f, toeplitz, sub_len, group_count):
    channels, total = values_f.shape
    reach_cols = FILT - 1
    count = total // sub_len
    padded = jnp.pad(values_f, ((0, 0), (reach_cols, 0)))
    lead = padded[:, :total].reshape(channels, count, sub_len)[:, :, :reach_cols]
    windows = jnp.concatenate([lead, values_f.reshape(channels, count, sub_len)], axis=2)
    windows = windows.reshape(group_count, channels // group_count, count, sub_len + reach_cols)
    out = jnp.einsum('gcns,gts->gcnt', windows, toeplitz).reshape(channels, total)
    return (out, windows)

def reference(outer_gate, inner_gate, value_stream, grad_output, filters, feature_taps, skip_gain):
    if LENGTH % FILT == 0:
        sub_len = FILT
    else:
        sub_len = min(TOK_DEV, 512)
    group_block = math.gcd(GROUPS, max(1, 128 // GROUP_SIZE))
    block_count = GROUPS // group_block
    chan_block = group_block * GROUP_SIZE

    def one_block(pieces):
        outer_b, inner_b, value_b, upstream_raw, filt_b, taps_b, skip_b = pieces
        toeplitz = toeplitz_rows(filt_b.astype(jnp.bfloat16), sub_len).astype(jnp.float32)
        outer_feat = featurize(outer_b, taps_b[0])
        inner_feat = featurize(inner_b, taps_b[1])
        value_feat = featurize(value_b, taps_b[2])
        product = (inner_feat * value_feat).astype(jnp.bfloat16)
        product_f = product.astype(jnp.float32)
        convolved, windows = causal_conv(product_f, toeplitz, sub_len, group_block)
        mixed = convolved + skip_b[:, None] * product_f
        gated_out = (outer_feat * mixed).astype(jnp.bfloat16)
        upstream = upstream_raw.astype(jnp.float32)
        grad_mixed = (upstream * outer_feat).astype(jnp.bfloat16)
        grad_outer_feat = (upstream * mixed).astype(jnp.bfloat16)
        grad_mixed_f = grad_mixed.astype(jnp.float32)
        reversed_out, unused = causal_conv(grad_mixed_f[:, ::-1], toeplitz, sub_len, group_block)
        grad_product = reversed_out[:, ::-1] + skip_b[:, None] * grad_mixed_f
        grad_inner_feat = (grad_product * value_feat).astype(jnp.bfloat16)
        grad_value_feat = (grad_product * inner_feat).astype(jnp.bfloat16)
        grad_outer = carry_back(grad_outer_feat, taps_b[0]).astype(jnp.bfloat16)
        grad_inner = carry_back(grad_inner_feat, taps_b[1]).astype(jnp.bfloat16)
        grad_value = carry_back(grad_value_feat, taps_b[2]).astype(jnp.bfloat16)
        grad_blocks = grad_mixed_f.reshape(group_block, GROUP_SIZE, LENGTH // sub_len, sub_len)
        cross_terms = jnp.einsum('gcnt,gcns->gts', grad_blocks, windows)
        filter_part = skew_sum(cross_terms, FILT)
        skip_part = lax.optimization_barrier(jnp.sum(grad_mixed_f * product_f, axis=1))
        taps_part = jnp.stack([tap_sums(grad_outer_feat, outer_b), tap_sums(grad_inner_feat, inner_b), tap_sums(grad_value_feat, value_b)])
        return (gated_out, grad_outer, grad_inner, grad_value, filter_part, taps_part, skip_part)
    pieces = (outer_gate.reshape(block_count, chan_block, LENGTH), inner_gate.reshape(block_count, chan_block, LENGTH), value_stream.reshape(block_count, chan_block, LENGTH), grad_output.reshape(block_count, chan_block, LENGTH), filters.reshape(block_count, group_block, FILT), feature_taps.reshape(3, 3, block_count, chan_block).transpose(2, 0, 1, 3), skip_gain.reshape(block_count, chan_block))
    results = lax.map(one_block, pieces)
    grad_scale = 1.0 / math.sqrt(LENGTH)
    grad_filters = grad_scale * results[4].reshape(GROUPS, FILT)
    grad_taps = grad_scale * results[5].transpose(1, 2, 0, 3).reshape(3, 3, CH)
    grad_skip = grad_scale * results[6].reshape(CH)
    return (results[0].reshape(CH, LENGTH), results[1].reshape(CH, LENGTH), results[2].reshape(CH, LENGTH), results[3].reshape(CH, LENGTH), grad_filters, grad_taps, grad_skip)
```

```python
import math

import jax
import jax.numpy as jnp
from jax import lax
from jax.sharding import PartitionSpec as P


def passed_along(shard, axis, by):
    devices = lax.axis_size(axis)
    pairs = [(i, i + by) for i in range(devices) if 0 <= i + by < devices]
    return lax.ppermute(shard, axis, pairs)


def featurize(extended, tap_gains):
    out_len = extended.shape[1] - 2
    result = tap_gains[0][:, None] * extended[:, 2:]
    result = result + tap_gains[1][:, None] * extended[:, 1 : out_len + 1]
    return result + tap_gains[2][:, None] * extended[:, :out_len]


def carry_back(extended, tap_gains):
    out_len = extended.shape[1] - 2
    result = tap_gains[0][:, None] * extended[:, :out_len]
    result = result + tap_gains[1][:, None] * extended[:, 1 : out_len + 1]
    return result + tap_gains[2][:, None] * extended[:, 2:]


def tap_sums(grad_rows, extended):
    block_len = grad_rows.shape[1]
    weighted = grad_rows.astype(jnp.float32)
    return jnp.stack(
        [
            jnp.sum(
                weighted * extended[:, 2 - shift_by : 2 - shift_by + block_len].astype(jnp.float32),
                axis=1,
            )
            for shift_by in range(3)
        ]
    )


def toeplitz_rows(filters_low, out_len):
    groups, taps_count = filters_low.shape
    window = out_len + taps_count - 1
    filter_row = jnp.concatenate(
        [filters_low[:, ::-1], jnp.zeros((groups, window + 1 - taps_count), filters_low.dtype)],
        axis=1,
    )
    flattened = jnp.tile(filter_row, (1, out_len))[:, : out_len * window]
    return flattened.reshape(groups, out_len, window)


def skew_sum(cross_terms, taps_count):
    groups, block_len, window = cross_terms.shape
    flattened = jnp.pad(cross_terms.reshape(groups, block_len * window), ((0, 0), (0, block_len)))
    return jnp.sum(flattened.reshape(groups, block_len, window + 1)[:, :, :taps_count], axis=1)[
        :, ::-1
    ]


def regroup_target(lin, fsdp_size):
    i, j = divmod(lin, fsdp_size)
    return (fsdp_size * (i % fsdp_size) + j) * fsdp_size + i // fsdp_size


def shards(outer_gate, inner_gate, value_stream, grad_output, filters, feature_taps, skip_gain):
    channels, block_len = outer_gate.shape
    ctx_size = lax.axis_size("ctx")
    fsdp_size = lax.axis_size("fsdp")
    n_dev = ctx_size * fsdp_size
    groups, taps_here = filters.shape
    taps_count = taps_here * ctx_size
    reach_cols = taps_count - 1
    group_size = channels // groups
    chunk = feature_taps.shape[2]

    param_pack = jnp.concatenate([feature_taps.reshape(-1), skip_gain])
    regrouped = lax.ppermute(
        param_pack,
        ("ctx", "fsdp"),
        [(k, regroup_target(k, fsdp_size)) for k in range(n_dev)],
    )
    row = jnp.concatenate([filters.reshape(-1), regrouped])
    gathered = lax.all_to_all(
        jnp.broadcast_to(row[None], (ctx_size, row.shape[0])), "ctx", 0, 0, tiled=True
    )
    n_filt = groups * taps_here
    filters_all = (
        gathered[:, :n_filt]
        .reshape(ctx_size, groups, taps_here)
        .transpose(1, 0, 2)
        .reshape(groups, taps_count)
    )
    taps_all = (
        gathered[:, n_filt : n_filt + 9 * chunk]
        .reshape(ctx_size, 3, 3, chunk)
        .transpose(1, 2, 0, 3)
        .reshape(3, 3, channels)
    )
    skip_all = gathered[:, n_filt + 9 * chunk :].reshape(channels)

    prev_rims = passed_along(
        (
            outer_gate[:, block_len - 2 :],
            inner_gate[:, block_len - reach_cols - 2 :],
            value_stream[:, block_len - reach_cols - 2 :],
        ),
        "ctx",
        1,
    )
    next_rims = passed_along(
        (
            grad_output[:, : reach_cols + 2],
            outer_gate[:, : reach_cols + 2],
            inner_gate[:, :2],
            value_stream[:, :2],
        ),
        "ctx",
        -1,
    )
    outer_ext = jnp.concatenate([prev_rims[0], outer_gate, next_rims[1]], axis=1)
    inner_ext = jnp.concatenate([prev_rims[1], inner_gate, next_rims[2]], axis=1)
    value_ext = jnp.concatenate([prev_rims[2], value_stream, next_rims[3]], axis=1)
    upstream = jnp.concatenate([grad_output, next_rims[0]], axis=1).astype(jnp.float32)

    outer_feat = featurize(outer_ext.astype(jnp.float32), taps_all[0])
    inner_feat = featurize(inner_ext.astype(jnp.float32), taps_all[1])
    value_feat = featurize(value_ext.astype(jnp.float32), taps_all[2])
    product = (inner_feat * value_feat).astype(jnp.bfloat16)

    out_len = block_len + 2
    toeplitz = toeplitz_rows(filters_all.astype(jnp.bfloat16), out_len)
    windows = product.reshape(groups, group_size, out_len + reach_cols)
    convolved = jnp.einsum(
        "gcs,gts->gct", windows, toeplitz, preferred_element_type=jnp.float32
    ).reshape(channels, out_len)
    product_here = product[:, reach_cols:].astype(jnp.float32)
    mixed = convolved + skip_all[:, None] * product_here
    gated_out = (outer_feat[:, :block_len] * mixed[:, :block_len]).astype(jnp.bfloat16)

    grad_mixed = (upstream * outer_feat).astype(jnp.bfloat16)
    grad_outer_feat = (upstream[:, :out_len] * mixed).astype(jnp.bfloat16)
    gm_windows = grad_mixed[:, : out_len + reach_cols].reshape(groups, group_size, out_len + reach_cols)
    ahead = jnp.einsum(
        "gcs,gts->gct", gm_windows, toeplitz[:, ::-1, ::-1], preferred_element_type=jnp.float32
    ).reshape(channels, out_len)
    grad_product = ahead + skip_all[:, None] * grad_mixed[:, :out_len].astype(jnp.float32)
    grad_inner_feat = (grad_product * value_feat[:, reach_cols:]).astype(jnp.bfloat16)
    grad_value_feat = (grad_product * inner_feat[:, reach_cols:]).astype(jnp.bfloat16)

    grad_outer = carry_back(grad_outer_feat.astype(jnp.float32), taps_all[0])
    grad_inner = carry_back(grad_inner_feat.astype(jnp.float32), taps_all[1])
    grad_value = carry_back(grad_value_feat.astype(jnp.float32), taps_all[2])

    grad_scale = 1.0 / math.sqrt(ctx_size * block_len)
    gm_here = grad_mixed[:, :block_len]
    cross_terms = jnp.einsum(
        "gct,gcs->gts",
        gm_here.reshape(groups, group_size, block_len),
        product[:, : block_len + reach_cols].reshape(groups, group_size, block_len + reach_cols),
        preferred_element_type=jnp.float32,
    )
    filter_part = grad_scale * skew_sum(cross_terms, taps_count)
    skip_part = grad_scale * jnp.sum(
        gm_here.astype(jnp.float32) * product_here[:, :block_len], axis=1
    )
    taps_part = grad_scale * jnp.stack(
        [
            tap_sums(grad_outer_feat[:, :block_len], outer_ext[:, : block_len + 2]),
            tap_sums(grad_inner_feat[:, :block_len], inner_ext[:, reach_cols : reach_cols + block_len + 2]),
            tap_sums(grad_value_feat[:, :block_len], value_ext[:, reach_cols : reach_cols + block_len + 2]),
        ]
    )

    send = jnp.concatenate(
        [
            filter_part.reshape(groups, ctx_size, taps_here).transpose(1, 0, 2).reshape(ctx_size, -1),
            taps_part.reshape(3, 3, ctx_size, chunk).transpose(2, 0, 1, 3).reshape(ctx_size, -1),
            skip_part.reshape(ctx_size, chunk),
        ],
        axis=1,
    )
    reduced = jnp.sum(lax.all_to_all(send, "ctx", 0, 0, tiled=True), axis=0)
    filter_share = reduced[:n_filt].reshape(groups, taps_here)
    back = lax.ppermute(
        reduced[n_filt:],
        ("ctx", "fsdp"),
        [(regroup_target(k, fsdp_size), k) for k in range(n_dev)],
    )
    taps_share = back[: 9 * chunk].reshape(3, 3, chunk)
    skip_share = back[9 * chunk :]
    return (
        gated_out,
        grad_outer.astype(jnp.bfloat16),
        grad_inner.astype(jnp.bfloat16),
        grad_value.astype(jnp.bfloat16),
        filter_share,
        taps_share,
        skip_share,
    )


def solution(mesh):
    return jax.shard_map(
        shards,
        mesh=mesh,
        in_specs=(
            P("fsdp", "ctx"),
            P("fsdp", "ctx"),
            P("fsdp", "ctx"),
            P("fsdp", "ctx"),
            P("fsdp", "ctx"),
            P(None, None, ("ctx", "fsdp")),
            P(("ctx", "fsdp")),
        ),
        out_specs=(
            P("fsdp", "ctx"),
            P("fsdp", "ctx"),
            P("fsdp", "ctx"),
            P("fsdp", "ctx"),
            P("fsdp", "ctx"),
            P(None, None, ("ctx", "fsdp")),
            P(("ctx", "fsdp")),
        ),
        check_vma=False,
    )
```

```python
import math

import jax
import jax.numpy as jnp
from jax import lax
from jax.sharding import PartitionSpec as P


def passed_along(shard, axis, by):
    devices = lax.axis_size(axis)
    pairs = [(i, i + by) for i in range(devices) if 0 <= i + by < devices]
    return lax.ppermute(shard, axis, pairs)


def featurize(extended, tap_gains):
    out_len = extended.shape[1] - 2
    result = tap_gains[0][:, None] * extended[:, 2:]
    result = result + tap_gains[1][:, None] * extended[:, 1 : out_len + 1]
    return result + tap_gains[2][:, None] * extended[:, :out_len]


def carry_back(extended, tap_gains):
    out_len = extended.shape[1] - 2
    result = tap_gains[0][:, None] * extended[:, :out_len]
    result = result + tap_gains[1][:, None] * extended[:, 1 : out_len + 1]
    return result + tap_gains[2][:, None] * extended[:, 2:]


def tap_sums(grad_rows, extended):
    block_len = grad_rows.shape[1]
    weighted = grad_rows.astype(jnp.float32)
    return jnp.stack(
        [
            jnp.sum(
                weighted * extended[:, 2 - shift_by : 2 - shift_by + block_len].astype(jnp.float32),
                axis=1,
            )
            for shift_by in range(3)
        ]
    )


def toeplitz_rows(filters_low, out_len):
    groups, taps_count = filters_low.shape
    window = out_len + taps_count - 1
    filter_row = jnp.concatenate(
        [filters_low[:, ::-1], jnp.zeros((groups, window + 1 - taps_count), filters_low.dtype)],
        axis=1,
    )
    flattened = jnp.tile(filter_row, (1, out_len))[:, : out_len * window]
    return flattened.reshape(groups, out_len, window)


def skew_sum(cross_terms, taps_count):
    groups, block_len, window = cross_terms.shape
    flattened = jnp.pad(cross_terms.reshape(groups, block_len * window), ((0, 0), (0, block_len)))
    return jnp.sum(flattened.reshape(groups, block_len, window + 1)[:, :, :taps_count], axis=1)[
        :, ::-1
    ]


def regroup_target(lin, fsdp_size):
    i, j = divmod(lin, fsdp_size)
    return (fsdp_size * (i % fsdp_size) + j) * fsdp_size + i // fsdp_size


def shards(outer_gate, inner_gate, value_stream, grad_output, filters, feature_taps, skip_gain):
    channels, block_len = outer_gate.shape
    ctx_size = lax.axis_size("ctx")
    fsdp_size = lax.axis_size("fsdp")
    n_dev = ctx_size * fsdp_size
    groups, taps_here = filters.shape
    taps_count = taps_here * ctx_size
    reach_cols = taps_count - 1
    group_size = channels // groups
    chunk = feature_taps.shape[2]

    param_pack = jnp.concatenate([feature_taps.reshape(-1), skip_gain])
    regrouped = lax.ppermute(
        param_pack,
        ("ctx", "fsdp"),
        [(k, regroup_target(k, fsdp_size)) for k in range(n_dev)],
    )
    row = jnp.concatenate([filters.reshape(-1), regrouped])
    gathered = lax.all_to_all(
        jnp.broadcast_to(row[None], (ctx_size, row.shape[0])), "ctx", 0, 0, tiled=True
    )
    n_filt = groups * taps_here
    filters_all = (
        gathered[:, :n_filt]
        .reshape(ctx_size, groups, taps_here)
        .transpose(1, 0, 2)
        .reshape(groups, taps_count)
    )
    taps_all = (
        gathered[:, n_filt : n_filt + 9 * chunk]
        .reshape(ctx_size, 3, 3, chunk)
        .transpose(1, 2, 0, 3)
        .reshape(3, 3, channels)
    )
    skip_all = gathered[:, n_filt + 9 * chunk :].reshape(channels)

    rim = reach_cols + 2
    prev_rim = passed_along(
        jnp.concatenate(
            [outer_gate[:, block_len - 2 :], inner_gate[:, block_len - rim :], value_stream[:, block_len - rim :]],
            axis=1,
        ),
        "ctx",
        1,
    )
    next_rim = passed_along(
        jnp.concatenate(
            [grad_output[:, :rim], outer_gate[:, :rim], inner_gate[:, :2], value_stream[:, :2]], axis=1
        ),
        "ctx",
        -1,
    )
    outer_ext = jnp.concatenate([prev_rim[:, :2], outer_gate, next_rim[:, rim : 2 * rim]], axis=1)
    inner_ext = jnp.concatenate(
        [prev_rim[:, 2 : 2 + rim], inner_gate, next_rim[:, 2 * rim : 2 * rim + 2]], axis=1
    )
    value_ext = jnp.concatenate([prev_rim[:, 2 + rim :], value_stream, next_rim[:, 2 * rim + 2 :]], axis=1)
    upstream = jnp.concatenate([grad_output, next_rim[:, :rim]], axis=1).astype(jnp.float32)

    outer_feat = featurize(outer_ext.astype(jnp.float32), taps_all[0])
    inner_feat = featurize(inner_ext.astype(jnp.float32), taps_all[1])
    value_feat = featurize(value_ext.astype(jnp.float32), taps_all[2])
    product = (inner_feat * value_feat).astype(jnp.bfloat16)

    out_len = block_len + 2
    toeplitz = toeplitz_rows(filters_all.astype(jnp.bfloat16), out_len)
    windows = product.reshape(groups, group_size, out_len + reach_cols)
    convolved = jnp.einsum(
        "gcs,gts->gct", windows, toeplitz, preferred_element_type=jnp.float32
    ).reshape(channels, out_len)
    product_here = product[:, reach_cols:].astype(jnp.float32)
    mixed = convolved + skip_all[:, None] * product_here
    gated_out = (outer_feat[:, :block_len] * mixed[:, :block_len]).astype(jnp.bfloat16)

    grad_mixed = (upstream * outer_feat).astype(jnp.bfloat16)
    grad_outer_feat = (upstream[:, :out_len] * mixed).astype(jnp.bfloat16)
    gm_windows = grad_mixed[:, ::-1].reshape(groups, group_size, out_len + reach_cols)
    ahead = jnp.einsum(
        "gcs,gts->gct", gm_windows, toeplitz, preferred_element_type=jnp.float32
    ).reshape(channels, out_len)[:, ::-1]
    grad_product = ahead + skip_all[:, None] * grad_mixed[:, :out_len].astype(jnp.float32)
    grad_inner_feat = (grad_product * value_feat[:, reach_cols:]).astype(jnp.bfloat16)
    grad_value_feat = (grad_product * inner_feat[:, reach_cols:]).astype(jnp.bfloat16)

    grad_outer = carry_back(grad_outer_feat.astype(jnp.float32), taps_all[0])
    grad_inner = carry_back(grad_inner_feat.astype(jnp.float32), taps_all[1])
    grad_value = carry_back(grad_value_feat.astype(jnp.float32), taps_all[2])

    grad_scale = 1.0 / math.sqrt(ctx_size * block_len)
    gm_here = grad_mixed[:, :block_len]
    cross_terms = jnp.einsum(
        "gct,gcs->gts",
        gm_here.reshape(groups, group_size, block_len),
        product[:, : block_len + reach_cols].reshape(groups, group_size, block_len + reach_cols),
        preferred_element_type=jnp.float32,
    )
    filter_part = grad_scale * skew_sum(cross_terms, taps_count)
    skip_part = grad_scale * jnp.sum(
        gm_here.astype(jnp.float32) * product_here[:, :block_len], axis=1
    )
    taps_part = grad_scale * jnp.stack(
        [
            tap_sums(grad_outer_feat[:, :block_len], outer_ext[:, : block_len + 2]),
            tap_sums(grad_inner_feat[:, :block_len], inner_ext[:, reach_cols : reach_cols + block_len + 2]),
            tap_sums(grad_value_feat[:, :block_len], value_ext[:, reach_cols : reach_cols + block_len + 2]),
        ]
    )

    send = jnp.concatenate(
        [
            filter_part.reshape(groups, ctx_size, taps_here).transpose(1, 0, 2).reshape(ctx_size, -1),
            taps_part.reshape(3, 3, ctx_size, chunk).transpose(2, 0, 1, 3).reshape(ctx_size, -1),
            skip_part.reshape(ctx_size, chunk),
        ],
        axis=1,
    )
    reduced = jnp.sum(lax.all_to_all(send, "ctx", 0, 0, tiled=True), axis=0)
    filter_share = reduced[:n_filt].reshape(groups, taps_here)
    back = lax.ppermute(
        reduced[n_filt:],
        ("ctx", "fsdp"),
        [(regroup_target(k, fsdp_size), k) for k in range(n_dev)],
    )
    taps_share = back[: 9 * chunk].reshape(3, 3, chunk)
    skip_share = back[9 * chunk :]
    return (
        gated_out,
        grad_outer.astype(jnp.bfloat16),
        grad_inner.astype(jnp.bfloat16),
        grad_value.astype(jnp.bfloat16),
        filter_share,
        taps_share,
        skip_share,
    )


def solution(mesh):
    return jax.shard_map(
        shards,
        mesh=mesh,
        in_specs=(
            P("fsdp", "ctx"),
            P("fsdp", "ctx"),
            P("fsdp", "ctx"),
            P("fsdp", "ctx"),
            P("fsdp", "ctx"),
            P(None, None, ("ctx", "fsdp")),
            P(("ctx", "fsdp")),
        ),
        out_specs=(
            P("fsdp", "ctx"),
            P("fsdp", "ctx"),
            P("fsdp", "ctx"),
            P("fsdp", "ctx"),
            P("fsdp", "ctx"),
            P(None, None, ("ctx", "fsdp")),
            P(("ctx", "fsdp")),
        ),
        check_vma=False,
    )
```

```python
import math

import jax
import jax.numpy as jnp
from jax import lax
from jax.sharding import PartitionSpec as P


def passed_along(shard, axis, by):
    devices = lax.axis_size(axis)
    pairs = [(i, i + by) for i in range(devices) if 0 <= i + by < devices]
    return lax.ppermute(shard, axis, pairs)


def featurize(extended, tap_gains):
    out_len = extended.shape[1] - 2
    result = tap_gains[0][:, None] * extended[:, 2:]
    result = result + tap_gains[1][:, None] * extended[:, 1 : out_len + 1]
    return result + tap_gains[2][:, None] * extended[:, :out_len]


def carry_back(extended, tap_gains):
    out_len = extended.shape[1] - 2
    result = tap_gains[0][:, None] * extended[:, :out_len]
    result = result + tap_gains[1][:, None] * extended[:, 1 : out_len + 1]
    return result + tap_gains[2][:, None] * extended[:, 2:]


def tap_sums(grad_rows, extended):
    block_len = grad_rows.shape[1]
    weighted = grad_rows.astype(jnp.float32)
    return jnp.stack(
        [
            jnp.sum(
                weighted * extended[:, 2 - shift_by : 2 - shift_by + block_len].astype(jnp.float32),
                axis=1,
            )
            for shift_by in range(3)
        ]
    )


def toeplitz_rows(filters_low, out_len):
    groups, taps_count = filters_low.shape
    window = out_len + taps_count - 1
    filter_row = jnp.concatenate(
        [filters_low[:, ::-1], jnp.zeros((groups, window + 1 - taps_count), filters_low.dtype)],
        axis=1,
    )
    flattened = jnp.tile(filter_row, (1, out_len))[:, : out_len * window]
    return flattened.reshape(groups, out_len, window)


def skew_sum(cross_terms, taps_count):
    groups, block_len, window = cross_terms.shape
    flattened = jnp.pad(cross_terms.reshape(groups, block_len * window), ((0, 0), (0, block_len)))
    return jnp.sum(flattened.reshape(groups, block_len, window + 1)[:, :, :taps_count], axis=1)[
        :, ::-1
    ]


def depthwise(values, kernel):
    channels = values.shape[0]
    return lax.conv_general_dilated(
        values[None],
        kernel[:, None, :],
        window_strides=(1,),
        padding="VALID",
        dimension_numbers=("NCH", "OIH", "NCH"),
        feature_group_count=channels,
        preferred_element_type=jnp.float32,
    )[0]


def regroup_target(lin, fsdp_size):
    i, j = divmod(lin, fsdp_size)
    return (fsdp_size * (i % fsdp_size) + j) * fsdp_size + i // fsdp_size


def shards(outer_gate, inner_gate, value_stream, grad_output, filters, feature_taps, skip_gain):
    channels, block_len = outer_gate.shape
    ctx_size = lax.axis_size("ctx")
    fsdp_size = lax.axis_size("fsdp")
    n_dev = ctx_size * fsdp_size
    groups, taps_here = filters.shape
    taps_count = taps_here * ctx_size
    reach_cols = taps_count - 1
    group_size = channels // groups
    chunk = feature_taps.shape[2]

    param_pack = jnp.concatenate([feature_taps.reshape(-1), skip_gain])
    regrouped = lax.ppermute(
        param_pack,
        ("ctx", "fsdp"),
        [(k, regroup_target(k, fsdp_size)) for k in range(n_dev)],
    )
    row = jnp.concatenate([filters.reshape(-1), regrouped])
    gathered = lax.all_to_all(
        jnp.broadcast_to(row[None], (ctx_size, row.shape[0])), "ctx", 0, 0, tiled=True
    )
    n_filt = groups * taps_here
    filters_all = (
        gathered[:, :n_filt]
        .reshape(ctx_size, groups, taps_here)
        .transpose(1, 0, 2)
        .reshape(groups, taps_count)
    )
    taps_all = (
        gathered[:, n_filt : n_filt + 9 * chunk]
        .reshape(ctx_size, 3, 3, chunk)
        .transpose(1, 2, 0, 3)
        .reshape(3, 3, channels)
    )
    skip_all = gathered[:, n_filt + 9 * chunk :].reshape(channels)

    rim = reach_cols + 2
    prev_rim = passed_along(
        jnp.concatenate(
            [outer_gate[:, block_len - 2 :], inner_gate[:, block_len - rim :], value_stream[:, block_len - rim :]],
            axis=1,
        ),
        "ctx",
        1,
    )
    next_rim = passed_along(
        jnp.concatenate(
            [grad_output[:, :rim], outer_gate[:, :rim], inner_gate[:, :2], value_stream[:, :2]], axis=1
        ),
        "ctx",
        -1,
    )
    outer_ext = jnp.concatenate([prev_rim[:, :2], outer_gate, next_rim[:, rim : 2 * rim]], axis=1)
    inner_ext = jnp.concatenate(
        [prev_rim[:, 2 : 2 + rim], inner_gate, next_rim[:, 2 * rim : 2 * rim + 2]], axis=1
    )
    value_ext = jnp.concatenate([prev_rim[:, 2 + rim :], value_stream, next_rim[:, 2 * rim + 2 :]], axis=1)
    upstream = jnp.concatenate([grad_output, next_rim[:, :rim]], axis=1).astype(jnp.float32)

    outer_feat = featurize(outer_ext.astype(jnp.float32), taps_all[0])
    inner_feat = featurize(inner_ext.astype(jnp.float32), taps_all[1])
    value_feat = featurize(value_ext.astype(jnp.float32), taps_all[2])
    product = (inner_feat * value_feat).astype(jnp.bfloat16)

    out_len = block_len + 2
    filters_low = filters_all.astype(jnp.bfloat16)
    per_channel = jnp.repeat(filters_low, group_size, axis=0)
    convolved = depthwise(product, per_channel[:, ::-1])
    product_here = product[:, reach_cols:].astype(jnp.float32)
    mixed = convolved + skip_all[:, None] * product_here
    gated_out = (outer_feat[:, :block_len] * mixed[:, :block_len]).astype(jnp.bfloat16)

    grad_mixed = (upstream * outer_feat).astype(jnp.bfloat16)
    grad_outer_feat = (upstream[:, :out_len] * mixed).astype(jnp.bfloat16)
    ahead = depthwise(grad_mixed, per_channel)
    grad_product = ahead + skip_all[:, None] * grad_mixed[:, :out_len].astype(jnp.float32)
    grad_inner_feat = (grad_product * value_feat[:, reach_cols:]).astype(jnp.bfloat16)
    grad_value_feat = (grad_product * inner_feat[:, reach_cols:]).astype(jnp.bfloat16)

    grad_outer = carry_back(grad_outer_feat.astype(jnp.float32), taps_all[0])
    grad_inner = carry_back(grad_inner_feat.astype(jnp.float32), taps_all[1])
    grad_value = carry_back(grad_value_feat.astype(jnp.float32), taps_all[2])

    grad_scale = 1.0 / math.sqrt(ctx_size * block_len)
    gm_here = grad_mixed[:, :block_len]
    filter_rev = depthwise(product[:, : block_len + reach_cols], gm_here)
    filter_part = grad_scale * jnp.sum(
        filter_rev.reshape(groups, group_size, taps_count), axis=1
    )[:, ::-1]
    skip_part = grad_scale * jnp.sum(
        gm_here.astype(jnp.float32) * product_here[:, :block_len], axis=1
    )
    taps_part = grad_scale * jnp.stack(
        [
            tap_sums(grad_outer_feat[:, :block_len], outer_ext[:, : block_len + 2]),
            tap_sums(grad_inner_feat[:, :block_len], inner_ext[:, reach_cols : reach_cols + block_len + 2]),
            tap_sums(grad_value_feat[:, :block_len], value_ext[:, reach_cols : reach_cols + block_len + 2]),
        ]
    )

    send = jnp.concatenate(
        [
            filter_part.reshape(groups, ctx_size, taps_here).transpose(1, 0, 2).reshape(ctx_size, -1),
            taps_part.reshape(3, 3, ctx_size, chunk).transpose(2, 0, 1, 3).reshape(ctx_size, -1),
            skip_part.reshape(ctx_size, chunk),
        ],
        axis=1,
    )
    reduced = jnp.sum(lax.all_to_all(send, "ctx", 0, 0, tiled=True), axis=0)
    filter_share = reduced[:n_filt].reshape(groups, taps_here)
    back = lax.ppermute(
        reduced[n_filt:],
        ("ctx", "fsdp"),
        [(regroup_target(k, fsdp_size), k) for k in range(n_dev)],
    )
    taps_share = back[: 9 * chunk].reshape(3, 3, chunk)
    skip_share = back[9 * chunk :]
    return (
        gated_out,
        grad_outer.astype(jnp.bfloat16),
        grad_inner.astype(jnp.bfloat16),
        grad_value.astype(jnp.bfloat16),
        filter_share,
        taps_share,
        skip_share,
    )


def solution(mesh):
    return jax.shard_map(
        shards,
        mesh=mesh,
        in_specs=(
            P("fsdp", "ctx"),
            P("fsdp", "ctx"),
            P("fsdp", "ctx"),
            P("fsdp", "ctx"),
            P("fsdp", "ctx"),
            P(None, None, ("ctx", "fsdp")),
            P(("ctx", "fsdp")),
        ),
        out_specs=(
            P("fsdp", "ctx"),
            P("fsdp", "ctx"),
            P("fsdp", "ctx"),
            P("fsdp", "ctx"),
            P("fsdp", "ctx"),
            P(None, None, ("ctx", "fsdp")),
            P(("ctx", "fsdp")),
        ),
        check_vma=False,
    )
```

```python
import math

import jax
import jax.numpy as jnp
from jax import lax
from jax.sharding import PartitionSpec as P


def passed_along(shard, axis, by):
    devices = lax.axis_size(axis)
    pairs = [(i, i + by) for i in range(devices) if 0 <= i + by < devices]
    return lax.ppermute(shard, axis, pairs)


def featurize(extended, tap_gains):
    out_len = extended.shape[1] - 2
    result = tap_gains[0][:, None] * extended[:, 2:]
    result = result + tap_gains[1][:, None] * extended[:, 1 : out_len + 1]
    return result + tap_gains[2][:, None] * extended[:, :out_len]


def carry_back(extended, tap_gains):
    out_len = extended.shape[1] - 2
    result = tap_gains[0][:, None] * extended[:, :out_len]
    result = result + tap_gains[1][:, None] * extended[:, 1 : out_len + 1]
    return result + tap_gains[2][:, None] * extended[:, 2:]


def tap_sums(grad_rows, extended):
    block_len = grad_rows.shape[1]
    weighted = grad_rows.astype(jnp.float32)
    return jnp.stack(
        [
            jnp.sum(
                weighted * extended[:, 2 - shift_by : 2 - shift_by + block_len].astype(jnp.float32),
                axis=1,
            )
            for shift_by in range(3)
        ]
    )


def toeplitz_rows(filters_low, out_len):
    groups, taps_count = filters_low.shape
    window = out_len + taps_count - 1
    filter_row = jnp.concatenate(
        [filters_low[:, ::-1], jnp.zeros((groups, window + 1 - taps_count), filters_low.dtype)],
        axis=1,
    )
    flattened = jnp.tile(filter_row, (1, out_len))[:, : out_len * window]
    return flattened.reshape(groups, out_len, window)


def skew_sum(cross_terms, taps_count):
    groups, block_len, window = cross_terms.shape
    flattened = jnp.pad(cross_terms.reshape(groups, block_len * window), ((0, 0), (0, block_len)))
    return jnp.sum(flattened.reshape(groups, block_len, window + 1)[:, :, :taps_count], axis=1)[
        :, ::-1
    ]


def depthwise(values, kernel):
    channels = values.shape[0]
    return lax.conv_general_dilated(
        values[None],
        kernel[:, None, :],
        window_strides=(1,),
        padding="VALID",
        dimension_numbers=("NCH", "OIH", "NCH"),
        feature_group_count=channels,
        preferred_element_type=jnp.float32,
    )[0]


def shards(outer_gate, inner_gate, value_stream, grad_output, filters, feature_taps, skip_gain):
    channels, block_len = outer_gate.shape
    ctx_size = lax.axis_size("ctx")
    fsdp_size = lax.axis_size("fsdp")
    n_dev = ctx_size * fsdp_size
    groups, taps_here = filters.shape
    taps_count = taps_here * ctx_size
    reach_cols = taps_count - 1
    group_size = channels // groups
    chunk = feature_taps.shape[2]

    row = jnp.concatenate([filters.reshape(-1), feature_taps.reshape(-1), skip_gain])
    gathered = lax.all_to_all(
        jnp.broadcast_to(row[None], (ctx_size, row.shape[0])), "ctx", 0, 0, tiled=True
    )
    n_filt = groups * taps_here
    n_chunk = row.shape[0] - n_filt
    per_block = ctx_size // fsdp_size
    filters_all = (
        gathered[:, :n_filt]
        .reshape(ctx_size, groups, taps_here)
        .transpose(1, 0, 2)
        .reshape(groups, taps_count)
    )
    moved = lax.all_to_all(gathered[:, n_filt:], "fsdp", 0, 0, tiled=True)
    local = (
        moved.reshape(fsdp_size, per_block, n_chunk).transpose(1, 0, 2).reshape(ctx_size, n_chunk)
    )
    taps_all = (
        local[:, : 9 * chunk].reshape(ctx_size, 3, 3, chunk).transpose(1, 2, 0, 3).reshape(3, 3, channels)
    )
    skip_all = local[:, 9 * chunk :].reshape(channels)

    rim = reach_cols + 2
    prev_rim = passed_along(
        jnp.concatenate(
            [outer_gate[:, block_len - 2 :], inner_gate[:, block_len - rim :], value_stream[:, block_len - rim :]],
            axis=1,
        ),
        "ctx",
        1,
    )
    next_rim = passed_along(
        jnp.concatenate(
            [grad_output[:, :rim], outer_gate[:, :rim], inner_gate[:, :2], value_stream[:, :2]], axis=1
        ),
        "ctx",
        -1,
    )
    outer_ext = jnp.concatenate([prev_rim[:, :2], outer_gate, next_rim[:, rim : 2 * rim]], axis=1)
    inner_ext = jnp.concatenate(
        [prev_rim[:, 2 : 2 + rim], inner_gate, next_rim[:, 2 * rim : 2 * rim + 2]], axis=1
    )
    value_ext = jnp.concatenate([prev_rim[:, 2 + rim :], value_stream, next_rim[:, 2 * rim + 2 :]], axis=1)
    upstream = jnp.concatenate([grad_output, next_rim[:, :rim]], axis=1).astype(jnp.float32)

    outer_feat = featurize(outer_ext.astype(jnp.float32), taps_all[0])
    inner_feat = featurize(inner_ext.astype(jnp.float32), taps_all[1])
    value_feat = featurize(value_ext.astype(jnp.float32), taps_all[2])
    product = (inner_feat * value_feat).astype(jnp.bfloat16)

    out_len = block_len + 2
    filters_low = filters_all.astype(jnp.bfloat16)
    per_channel = jnp.repeat(filters_low, group_size, axis=0)
    convolved = depthwise(product, per_channel[:, ::-1])
    product_here = product[:, reach_cols:].astype(jnp.float32)
    mixed = convolved + skip_all[:, None] * product_here
    gated_out = (outer_feat[:, :block_len] * mixed[:, :block_len]).astype(jnp.bfloat16)

    grad_mixed = (upstream * outer_feat).astype(jnp.bfloat16)
    grad_outer_feat = (upstream[:, :out_len] * mixed).astype(jnp.bfloat16)
    ahead = depthwise(grad_mixed, per_channel)
    grad_product = ahead + skip_all[:, None] * grad_mixed[:, :out_len].astype(jnp.float32)
    grad_inner_feat = (grad_product * value_feat[:, reach_cols:]).astype(jnp.bfloat16)
    grad_value_feat = (grad_product * inner_feat[:, reach_cols:]).astype(jnp.bfloat16)

    grad_outer = carry_back(grad_outer_feat.astype(jnp.float32), taps_all[0])
    grad_inner = carry_back(grad_inner_feat.astype(jnp.float32), taps_all[1])
    grad_value = carry_back(grad_value_feat.astype(jnp.float32), taps_all[2])

    grad_scale = 1.0 / math.sqrt(ctx_size * block_len)
    gm_here = grad_mixed[:, :block_len]
    filter_rev = depthwise(product[:, : block_len + reach_cols], gm_here)
    filter_part = grad_scale * jnp.sum(
        filter_rev.reshape(groups, group_size, taps_count), axis=1
    )[:, ::-1]
    skip_part = grad_scale * jnp.sum(
        gm_here.astype(jnp.float32) * product_here[:, :block_len], axis=1
    )
    taps_part = grad_scale * jnp.stack(
        [
            tap_sums(grad_outer_feat[:, :block_len], outer_ext[:, : block_len + 2]),
            tap_sums(grad_inner_feat[:, :block_len], inner_ext[:, reach_cols : reach_cols + block_len + 2]),
            tap_sums(grad_value_feat[:, :block_len], value_ext[:, reach_cols : reach_cols + block_len + 2]),
        ]
    )

    chunk_parts = jnp.concatenate(
        [
            taps_part.reshape(3, 3, ctx_size, chunk).transpose(2, 0, 1, 3).reshape(ctx_size, -1),
            skip_part.reshape(ctx_size, chunk),
        ],
        axis=1,
    )
    to_fsdp = chunk_parts.reshape(per_block, fsdp_size, n_chunk).transpose(1, 0, 2).reshape(ctx_size, n_chunk)
    by_owner = lax.all_to_all(to_fsdp, "fsdp", 0, 0, tiled=True)
    send = jnp.concatenate(
        [
            filter_part.reshape(groups, ctx_size, taps_here).transpose(1, 0, 2).reshape(ctx_size, -1),
            by_owner,
        ],
        axis=1,
    )
    reduced = jnp.sum(lax.all_to_all(send, "ctx", 0, 0, tiled=True), axis=0)
    filter_share = reduced[:n_filt].reshape(groups, taps_here)
    taps_share = reduced[n_filt : n_filt + 9 * chunk].reshape(3, 3, chunk)
    skip_share = reduced[n_filt + 9 * chunk :]
    return (
        gated_out,
        grad_outer.astype(jnp.bfloat16),
        grad_inner.astype(jnp.bfloat16),
        grad_value.astype(jnp.bfloat16),
        filter_share,
        taps_share,
        skip_share,
    )


def solution(mesh):
    return jax.shard_map(
        shards,
        mesh=mesh,
        in_specs=(
            P("fsdp", "ctx"),
            P("fsdp", "ctx"),
            P("fsdp", "ctx"),
            P("fsdp", "ctx"),
            P("fsdp", "ctx"),
            P(None, None, ("ctx", "fsdp")),
            P(("ctx", "fsdp")),
        ),
        out_specs=(
            P("fsdp", "ctx"),
            P("fsdp", "ctx"),
            P("fsdp", "ctx"),
            P("fsdp", "ctx"),
            P("fsdp", "ctx"),
            P(None, None, ("ctx", "fsdp")),
            P(("ctx", "fsdp")),
        ),
        check_vma=False,
    )
```

```python
import math

import jax
import jax.numpy as jnp
from jax import lax
from jax.experimental import pallas as pl
from jax.experimental.pallas import tpu as pltpu
from jax.sharding import PartitionSpec as P


def passed_along(shard, axis, by):
    devices = lax.axis_size(axis)
    pairs = [(i, i + by) for i in range(devices) if 0 <= i + by < devices]
    return lax.ppermute(shard, axis, pairs)


def featurize(extended, tap_gains):
    out_len = extended.shape[1] - 2
    result = tap_gains[0][:, None] * extended[:, 2:]
    result = result + tap_gains[1][:, None] * extended[:, 1 : out_len + 1]
    return result + tap_gains[2][:, None] * extended[:, :out_len]


def carry_back(extended, tap_gains):
    out_len = extended.shape[1] - 2
    result = tap_gains[0][:, None] * extended[:, :out_len]
    result = result + tap_gains[1][:, None] * extended[:, 1 : out_len + 1]
    return result + tap_gains[2][:, None] * extended[:, 2:]


def tap_sums(grad_rows, extended):
    block_len = grad_rows.shape[1]
    weighted = grad_rows.astype(jnp.float32)
    return jnp.stack(
        [
            jnp.sum(
                weighted * extended[:, 2 - shift_by : 2 - shift_by + block_len].astype(jnp.float32),
                axis=1,
            )
            for shift_by in range(3)
        ]
    )


def toeplitz_rows(filters_low, out_len):
    groups, taps_count = filters_low.shape
    window = out_len + taps_count - 1
    filter_row = jnp.concatenate(
        [filters_low[:, ::-1], jnp.zeros((groups, window + 1 - taps_count), filters_low.dtype)],
        axis=1,
    )
    flattened = jnp.tile(filter_row, (1, out_len))[:, : out_len * window]
    return flattened.reshape(groups, out_len, window)


def skew_sum(cross_terms, taps_count):
    groups, block_len, window = cross_terms.shape
    flattened = jnp.pad(cross_terms.reshape(groups, block_len * window), ((0, 0), (0, block_len)))
    return jnp.sum(flattened.reshape(groups, block_len, window + 1)[:, :, :taps_count], axis=1)[
        :, ::-1
    ]


def depthwise(values, kernel):
    channels = values.shape[0]
    return lax.conv_general_dilated(
        values[None],
        kernel[:, None, :],
        window_strides=(1,),
        padding="VALID",
        dimension_numbers=("NCH", "OIH", "NCH"),
        feature_group_count=channels,
        preferred_element_type=jnp.float32,
    )[0]


def banded_kernel(ahead_ref, behind_ref, pw_ref, gw_ref, fo_ref, bo_ref):
    rows = fo_ref.shape[2]
    lanes = ahead_ref.shape[1]
    dims = (((1,), (1,)), ((), ()))
    for group in range(ahead_ref.shape[0]):
        for row_ref, data_ref, out_ref in ((ahead_ref, pw_ref, fo_ref), (behind_ref, gw_ref, bo_ref)):
            band = pltpu.roll(
                jnp.broadcast_to(row_ref[group : group + 1, :], (rows, lanes)), 0, 1, stride=1, stride_axis=0
            ).astype(jnp.bfloat16)
            out_ref[group] = lax.dot_general(
                data_ref[group], band, dims, preferred_element_type=jnp.float32
            )


def both_convs(product, grad_mixed, filters_low):
    channels, win = product.shape
    groups, taps = filters_low.shape
    out_len = win - taps + 1
    rows = -(-out_len // 16) * 16
    lanes = -(-max(win, rows + taps - 1) // 128) * 128
    as_rows = filters_low.astype(jnp.float32)
    ahead = jnp.pad(as_rows[:, ::-1], ((0, 0), (0, lanes - taps)))
    behind = jnp.pad(as_rows, ((0, 0), (0, lanes - taps)))
    pw = jnp.pad(product, ((0, 0), (0, lanes - win))).reshape(groups, channels // groups, lanes)
    gw = jnp.pad(grad_mixed, ((0, 0), (0, lanes - win))).reshape(groups, channels // groups, lanes)
    spec = pl.BlockSpec(memory_space=pltpu.VMEM)
    fo, bo = pl.pallas_call(
        banded_kernel,
        out_shape=(jax.ShapeDtypeStruct((groups, channels // groups, rows), jnp.float32),) * 2,
        in_specs=[spec] * 4,
        out_specs=(spec, spec),
        cost_estimate=pl.CostEstimate(
            flops=4 * channels * lanes * rows, transcendentals=0, bytes_accessed=4 * channels * (lanes + 2 * rows)
        ),
    )(ahead, behind, pw, gw)
    return fo.reshape(channels, rows)[:, :out_len], bo.reshape(channels, rows)[:, :out_len]


def shards(outer_gate, inner_gate, value_stream, grad_output, filters, feature_taps, skip_gain):
    channels, block_len = outer_gate.shape
    ctx_size = lax.axis_size("ctx")
    fsdp_size = lax.axis_size("fsdp")
    n_dev = ctx_size * fsdp_size
    groups, taps_here = filters.shape
    taps_count = taps_here * ctx_size
    reach_cols = taps_count - 1
    group_size = channels // groups
    chunk = feature_taps.shape[2]

    row = jnp.concatenate([filters.reshape(-1), feature_taps.reshape(-1), skip_gain])
    gathered = lax.all_to_all(
        jnp.broadcast_to(row[None], (ctx_size, row.shape[0])), "ctx", 0, 0, tiled=True
    )
    n_filt = groups * taps_here
    n_chunk = row.shape[0] - n_filt
    per_block = ctx_size // fsdp_size
    filters_all = (
        gathered[:, :n_filt]
        .reshape(ctx_size, groups, taps_here)
        .transpose(1, 0, 2)
        .reshape(groups, taps_count)
    )
    moved = lax.all_to_all(gathered[:, n_filt:], "fsdp", 0, 0, tiled=True)
    local = (
        moved.reshape(fsdp_size, per_block, n_chunk).transpose(1, 0, 2).reshape(ctx_size, n_chunk)
    )
    taps_all = (
        local[:, : 9 * chunk].reshape(ctx_size, 3, 3, chunk).transpose(1, 2, 0, 3).reshape(3, 3, channels)
    )
    skip_all = local[:, 9 * chunk :].reshape(channels)

    rim = reach_cols + 2
    prev_rim = passed_along(
        jnp.concatenate(
            [outer_gate[:, block_len - 2 :], inner_gate[:, block_len - rim :], value_stream[:, block_len - rim :]],
            axis=1,
        ),
        "ctx",
        1,
    )
    next_rim = passed_along(
        jnp.concatenate(
            [grad_output[:, :rim], outer_gate[:, :rim], inner_gate[:, :2], value_stream[:, :2]], axis=1
        ),
        "ctx",
        -1,
    )
    outer_ext = jnp.concatenate([prev_rim[:, :2], outer_gate, next_rim[:, rim : 2 * rim]], axis=1)
    inner_ext = jnp.concatenate(
        [prev_rim[:, 2 : 2 + rim], inner_gate, next_rim[:, 2 * rim : 2 * rim + 2]], axis=1
    )
    value_ext = jnp.concatenate([prev_rim[:, 2 + rim :], value_stream, next_rim[:, 2 * rim + 2 :]], axis=1)
    upstream = jnp.concatenate([grad_output, next_rim[:, :rim]], axis=1).astype(jnp.float32)

    outer_feat = featurize(outer_ext.astype(jnp.float32), taps_all[0])
    inner_feat = featurize(inner_ext.astype(jnp.float32), taps_all[1])
    value_feat = featurize(value_ext.astype(jnp.float32), taps_all[2])
    product = (inner_feat * value_feat).astype(jnp.bfloat16)

    out_len = block_len + 2
    filters_low = filters_all.astype(jnp.bfloat16)
    product_here = product[:, reach_cols:].astype(jnp.float32)
    grad_mixed = (upstream * outer_feat).astype(jnp.bfloat16)
    convolved, ahead = both_convs(product, grad_mixed, filters_low)
    mixed = convolved + skip_all[:, None] * product_here
    gated_out = (outer_feat[:, :block_len] * mixed[:, :block_len]).astype(jnp.bfloat16)

    grad_outer_feat = (upstream[:, :out_len] * mixed).astype(jnp.bfloat16)
    grad_product = ahead + skip_all[:, None] * grad_mixed[:, :out_len].astype(jnp.float32)
    grad_inner_feat = (grad_product * value_feat[:, reach_cols:]).astype(jnp.bfloat16)
    grad_value_feat = (grad_product * inner_feat[:, reach_cols:]).astype(jnp.bfloat16)

    grad_outer = carry_back(grad_outer_feat.astype(jnp.float32), taps_all[0])
    grad_inner = carry_back(grad_inner_feat.astype(jnp.float32), taps_all[1])
    grad_value = carry_back(grad_value_feat.astype(jnp.float32), taps_all[2])

    grad_scale = 1.0 / math.sqrt(ctx_size * block_len)
    gm_here = grad_mixed[:, :block_len]
    filter_rev = depthwise(product[:, : block_len + reach_cols], gm_here)
    filter_part = grad_scale * jnp.sum(
        filter_rev.reshape(groups, group_size, taps_count), axis=1
    )[:, ::-1]
    skip_part = grad_scale * jnp.sum(
        gm_here.astype(jnp.float32) * product_here[:, :block_len], axis=1
    )
    taps_part = grad_scale * jnp.stack(
        [
            tap_sums(grad_outer_feat[:, :block_len], outer_ext[:, : block_len + 2]),
            tap_sums(grad_inner_feat[:, :block_len], inner_ext[:, reach_cols : reach_cols + block_len + 2]),
            tap_sums(grad_value_feat[:, :block_len], value_ext[:, reach_cols : reach_cols + block_len + 2]),
        ]
    )

    chunk_parts = jnp.concatenate(
        [
            taps_part.reshape(3, 3, ctx_size, chunk).transpose(2, 0, 1, 3).reshape(ctx_size, -1),
            skip_part.reshape(ctx_size, chunk),
        ],
        axis=1,
    )
    to_fsdp = chunk_parts.reshape(per_block, fsdp_size, n_chunk).transpose(1, 0, 2).reshape(ctx_size, n_chunk)
    by_owner = lax.all_to_all(to_fsdp, "fsdp", 0, 0, tiled=True)
    send = jnp.concatenate(
        [
            filter_part.reshape(groups, ctx_size, taps_here).transpose(1, 0, 2).reshape(ctx_size, -1),
            by_owner,
        ],
        axis=1,
    )
    reduced = jnp.sum(lax.all_to_all(send, "ctx", 0, 0, tiled=True), axis=0)
    filter_share = reduced[:n_filt].reshape(groups, taps_here)
    taps_share = reduced[n_filt : n_filt + 9 * chunk].reshape(3, 3, chunk)
    skip_share = reduced[n_filt + 9 * chunk :]
    return (
        gated_out,
        grad_outer.astype(jnp.bfloat16),
        grad_inner.astype(jnp.bfloat16),
        grad_value.astype(jnp.bfloat16),
        filter_share,
        taps_share,
        skip_share,
    )


def solution(mesh):
    return jax.shard_map(
        shards,
        mesh=mesh,
        in_specs=(
            P("fsdp", "ctx"),
            P("fsdp", "ctx"),
            P("fsdp", "ctx"),
            P("fsdp", "ctx"),
            P("fsdp", "ctx"),
            P(None, None, ("ctx", "fsdp")),
            P(("ctx", "fsdp")),
        ),
        out_specs=(
            P("fsdp", "ctx"),
            P("fsdp", "ctx"),
            P("fsdp", "ctx"),
            P("fsdp", "ctx"),
            P("fsdp", "ctx"),
            P(None, None, ("ctx", "fsdp")),
            P(("ctx", "fsdp")),
        ),
        check_vma=False,
    )
```

```python
import functools
import math

import jax
import jax.numpy as jnp
from jax import lax
from jax.experimental import pallas as pl
from jax.experimental.pallas import tpu as pltpu
from jax.sharding import PartitionSpec as P


def passed_along(shard, axis, by):
    devices = lax.axis_size(axis)
    pairs = [(i, i + by) for i in range(devices) if 0 <= i + by < devices]
    return lax.ppermute(shard, axis, pairs)


def featurize(extended, tap_gains):
    out_len = extended.shape[1] - 2
    result = tap_gains[0][:, None] * extended[:, 2:]
    result = result + tap_gains[1][:, None] * extended[:, 1 : out_len + 1]
    return result + tap_gains[2][:, None] * extended[:, :out_len]


def carry_back(extended, tap_gains):
    out_len = extended.shape[1] - 2
    result = tap_gains[0][:, None] * extended[:, :out_len]
    result = result + tap_gains[1][:, None] * extended[:, 1 : out_len + 1]
    return result + tap_gains[2][:, None] * extended[:, 2:]


def tap_sums(grad_rows, extended):
    block_len = grad_rows.shape[1]
    weighted = grad_rows.astype(jnp.float32)
    return jnp.stack(
        [
            jnp.sum(
                weighted * extended[:, 2 - shift_by : 2 - shift_by + block_len].astype(jnp.float32),
                axis=1,
            )
            for shift_by in range(3)
        ]
    )


def toeplitz_rows(filters_low, out_len):
    groups, taps_count = filters_low.shape
    window = out_len + taps_count - 1
    filter_row = jnp.concatenate(
        [filters_low[:, ::-1], jnp.zeros((groups, window + 1 - taps_count), filters_low.dtype)],
        axis=1,
    )
    flattened = jnp.tile(filter_row, (1, out_len))[:, : out_len * window]
    return flattened.reshape(groups, out_len, window)


def skew_sum(cross_terms, taps_count):
    groups, block_len, window = cross_terms.shape
    flattened = jnp.pad(cross_terms.reshape(groups, block_len * window), ((0, 0), (0, block_len)))
    return jnp.sum(flattened.reshape(groups, block_len, window + 1)[:, :, :taps_count], axis=1)[
        :, ::-1
    ]


def depthwise(values, kernel):
    channels = values.shape[0]
    return lax.conv_general_dilated(
        values[None],
        kernel[:, None, :],
        window_strides=(1,),
        padding="VALID",
        dimension_numbers=("NCH", "OIH", "NCH"),
        feature_group_count=channels,
        preferred_element_type=jnp.float32,
    )[0]


def banded_kernel(ahead_ref, behind_ref, pw_ref, gw_ref, fo_ref, bo_ref, fg_ref, *, here):
    rows = fo_ref.shape[2]
    lanes = ahead_ref.shape[1]
    dims = (((1,), (1,)), ((), ()))
    flip = (
        lax.broadcasted_iota(jnp.int32, (here, here), 0) + lax.broadcasted_iota(jnp.int32, (here, here), 1)
        == here - 1
    ).astype(jnp.bfloat16)
    for group in range(ahead_ref.shape[0]):
        for row_ref, data_ref, out_ref in ((ahead_ref, pw_ref, fo_ref), (behind_ref, gw_ref, bo_ref)):
            band = pltpu.roll(
                jnp.broadcast_to(row_ref[group : group + 1, :], (rows, lanes)), 0, 1, stride=1, stride_axis=0
            ).astype(jnp.bfloat16)
            out_ref[group] = lax.dot_general(
                data_ref[group], band, dims, preferred_element_type=jnp.float32
            )
        gm_rev = jnp.dot(gw_ref[group][:, :here], flip, preferred_element_type=jnp.float32).astype(jnp.bfloat16)
        cross = lax.dot_general(
            gm_rev, pw_ref[group], (((0,), (0,)), ((), ())), preferred_element_type=jnp.float32
        )
        diag = pltpu.roll(cross, lanes - here + 1, 1, stride=1, stride_axis=0)
        fg_ref[group : group + 1, :] = jnp.sum(diag, axis=0, keepdims=True)[:, : fg_ref.shape[1]]


def both_convs(product, grad_mixed, filters_low, here):
    channels, win = product.shape
    groups, taps = filters_low.shape
    out_len = win - taps + 1
    rows = -(-out_len // 16) * 16
    lanes = -(-max(win, rows + taps - 1) // 128) * 128
    as_rows = filters_low.astype(jnp.float32)
    ahead = jnp.pad(as_rows[:, ::-1], ((0, 0), (0, lanes - taps)))
    behind = jnp.pad(as_rows, ((0, 0), (0, lanes - taps)))
    pw = jnp.pad(product, ((0, 0), (0, lanes - win))).reshape(groups, channels // groups, lanes)
    gw = jnp.pad(grad_mixed, ((0, 0), (0, lanes - win))).reshape(groups, channels // groups, lanes)
    spec = pl.BlockSpec(memory_space=pltpu.VMEM)
    fo, bo, fg = pl.pallas_call(
        functools.partial(banded_kernel, here=here),
        out_shape=(jax.ShapeDtypeStruct((groups, channels // groups, rows), jnp.float32),) * 2
        + (jax.ShapeDtypeStruct((groups, taps), jnp.float32),),
        in_specs=[spec] * 4,
        out_specs=(spec, spec, spec),
        cost_estimate=pl.CostEstimate(
            flops=4 * channels * lanes * (rows + here), transcendentals=0, bytes_accessed=4 * channels * (lanes + 2 * rows)
        ),
    )(ahead, behind, pw, gw)
    return fo.reshape(channels, rows)[:, :out_len], bo.reshape(channels, rows)[:, :out_len], fg


def shards(outer_gate, inner_gate, value_stream, grad_output, filters, feature_taps, skip_gain):
    channels, block_len = outer_gate.shape
    ctx_size = lax.axis_size("ctx")
    fsdp_size = lax.axis_size("fsdp")
    n_dev = ctx_size * fsdp_size
    groups, taps_here = filters.shape
    taps_count = taps_here * ctx_size
    reach_cols = taps_count - 1
    group_size = channels // groups
    chunk = feature_taps.shape[2]

    row = jnp.concatenate([filters.reshape(-1), feature_taps.reshape(-1), skip_gain])
    gathered = lax.all_to_all(
        jnp.broadcast_to(row[None], (ctx_size, row.shape[0])), "ctx", 0, 0, tiled=True
    )
    n_filt = groups * taps_here
    n_chunk = row.shape[0] - n_filt
    per_block = ctx_size // fsdp_size
    filters_all = (
        gathered[:, :n_filt]
        .reshape(ctx_size, groups, taps_here)
        .transpose(1, 0, 2)
        .reshape(groups, taps_count)
    )
    moved = lax.all_to_all(gathered[:, n_filt:], "fsdp", 0, 0, tiled=True)
    local = (
        moved.reshape(fsdp_size, per_block, n_chunk).transpose(1, 0, 2).reshape(ctx_size, n_chunk)
    )
    taps_all = (
        local[:, : 9 * chunk].reshape(ctx_size, 3, 3, chunk).transpose(1, 2, 0, 3).reshape(3, 3, channels)
    )
    skip_all = local[:, 9 * chunk :].reshape(channels)

    rim = reach_cols + 2
    prev_rim = passed_along(
        jnp.concatenate(
            [outer_gate[:, block_len - 2 :], inner_gate[:, block_len - rim :], value_stream[:, block_len - rim :]],
            axis=1,
        ),
        "ctx",
        1,
    )
    next_rim = passed_along(
        jnp.concatenate(
            [grad_output[:, :rim], outer_gate[:, :rim], inner_gate[:, :2], value_stream[:, :2]], axis=1
        ),
        "ctx",
        -1,
    )
    outer_ext = jnp.concatenate([prev_rim[:, :2], outer_gate, next_rim[:, rim : 2 * rim]], axis=1)
    inner_ext = jnp.concatenate(
        [prev_rim[:, 2 : 2 + rim], inner_gate, next_rim[:, 2 * rim : 2 * rim + 2]], axis=1
    )
    value_ext = jnp.concatenate([prev_rim[:, 2 + rim :], value_stream, next_rim[:, 2 * rim + 2 :]], axis=1)
    upstream = jnp.concatenate([grad_output, next_rim[:, :rim]], axis=1).astype(jnp.float32)

    outer_feat = featurize(outer_ext.astype(jnp.float32), taps_all[0])
    inner_feat = featurize(inner_ext.astype(jnp.float32), taps_all[1])
    value_feat = featurize(value_ext.astype(jnp.float32), taps_all[2])
    product = (inner_feat * value_feat).astype(jnp.bfloat16)

    out_len = block_len + 2
    filters_low = filters_all.astype(jnp.bfloat16)
    product_here = product[:, reach_cols:].astype(jnp.float32)
    grad_mixed = (upstream * outer_feat).astype(jnp.bfloat16)
    convolved, ahead, filter_diag = both_convs(product, grad_mixed, filters_low, block_len)
    mixed = convolved + skip_all[:, None] * product_here
    gated_out = (outer_feat[:, :block_len] * mixed[:, :block_len]).astype(jnp.bfloat16)

    grad_outer_feat = (upstream[:, :out_len] * mixed).astype(jnp.bfloat16)
    grad_product = ahead + skip_all[:, None] * grad_mixed[:, :out_len].astype(jnp.float32)
    grad_inner_feat = (grad_product * value_feat[:, reach_cols:]).astype(jnp.bfloat16)
    grad_value_feat = (grad_product * inner_feat[:, reach_cols:]).astype(jnp.bfloat16)

    grad_outer = carry_back(grad_outer_feat.astype(jnp.float32), taps_all[0])
    grad_inner = carry_back(grad_inner_feat.astype(jnp.float32), taps_all[1])
    grad_value = carry_back(grad_value_feat.astype(jnp.float32), taps_all[2])

    grad_scale = 1.0 / math.sqrt(ctx_size * block_len)
    gm_here = grad_mixed[:, :block_len]
    filter_part = grad_scale * filter_diag[:, ::-1]
    skip_part = grad_scale * jnp.sum(
        gm_here.astype(jnp.float32) * product_here[:, :block_len], axis=1
    )
    taps_part = grad_scale * jnp.stack(
        [
            tap_sums(grad_outer_feat[:, :block_len], outer_ext[:, : block_len + 2]),
            tap_sums(grad_inner_feat[:, :block_len], inner_ext[:, reach_cols : reach_cols + block_len + 2]),
            tap_sums(grad_value_feat[:, :block_len], value_ext[:, reach_cols : reach_cols + block_len + 2]),
        ]
    )

    chunk_parts = jnp.concatenate(
        [
            taps_part.reshape(3, 3, ctx_size, chunk).transpose(2, 0, 1, 3).reshape(ctx_size, -1),
            skip_part.reshape(ctx_size, chunk),
        ],
        axis=1,
    )
    to_fsdp = chunk_parts.reshape(per_block, fsdp_size, n_chunk).transpose(1, 0, 2).reshape(ctx_size, n_chunk)
    by_owner = lax.all_to_all(to_fsdp, "fsdp", 0, 0, tiled=True)
    send = jnp.concatenate(
        [
            filter_part.reshape(groups, ctx_size, taps_here).transpose(1, 0, 2).reshape(ctx_size, -1),
            by_owner,
        ],
        axis=1,
    )
    reduced = jnp.sum(lax.all_to_all(send, "ctx", 0, 0, tiled=True), axis=0)
    filter_share = reduced[:n_filt].reshape(groups, taps_here)
    taps_share = reduced[n_filt : n_filt + 9 * chunk].reshape(3, 3, chunk)
    skip_share = reduced[n_filt + 9 * chunk :]
    return (
        gated_out,
        grad_outer.astype(jnp.bfloat16),
        grad_inner.astype(jnp.bfloat16),
        grad_value.astype(jnp.bfloat16),
        filter_share,
        taps_share,
        skip_share,
    )


def solution(mesh):
    return jax.shard_map(
        shards,
        mesh=mesh,
        in_specs=(
            P("fsdp", "ctx"),
            P("fsdp", "ctx"),
            P("fsdp", "ctx"),
            P("fsdp", "ctx"),
            P("fsdp", "ctx"),
            P(None, None, ("ctx", "fsdp")),
            P(("ctx", "fsdp")),
        ),
        out_specs=(
            P("fsdp", "ctx"),
            P("fsdp", "ctx"),
            P("fsdp", "ctx"),
            P("fsdp", "ctx"),
            P("fsdp", "ctx"),
            P(None, None, ("ctx", "fsdp")),
            P(("ctx", "fsdp")),
        ),
        check_vma=False,
    )
```

```python
import functools
import math

import jax
import jax.numpy as jnp
from jax import lax
from jax.experimental import pallas as pl
from jax.experimental.pallas import tpu as pltpu
from jax.sharding import PartitionSpec as P


def passed_along(shard, axis, by):
    devices = lax.axis_size(axis)
    pairs = [(i, i + by) for i in range(devices) if 0 <= i + by < devices]
    return lax.ppermute(shard, axis, pairs)


def featurize(extended, tap_gains):
    out_len = extended.shape[1] - 2
    result = tap_gains[0][:, None] * extended[:, 2:]
    result = result + tap_gains[1][:, None] * extended[:, 1 : out_len + 1]
    return result + tap_gains[2][:, None] * extended[:, :out_len]


def carry_back(extended, tap_gains):
    out_len = extended.shape[1] - 2
    result = tap_gains[0][:, None] * extended[:, :out_len]
    result = result + tap_gains[1][:, None] * extended[:, 1 : out_len + 1]
    return result + tap_gains[2][:, None] * extended[:, 2:]


def tap_sums(grad_rows, extended):
    block_len = grad_rows.shape[1]
    weighted = grad_rows.astype(jnp.float32)
    return jnp.stack(
        [
            jnp.sum(
                weighted * extended[:, 2 - shift_by : 2 - shift_by + block_len].astype(jnp.float32),
                axis=1,
            )
            for shift_by in range(3)
        ]
    )


def toeplitz_rows(filters_low, out_len):
    groups, taps_count = filters_low.shape
    window = out_len + taps_count - 1
    filter_row = jnp.concatenate(
        [filters_low[:, ::-1], jnp.zeros((groups, window + 1 - taps_count), filters_low.dtype)],
        axis=1,
    )
    flattened = jnp.tile(filter_row, (1, out_len))[:, : out_len * window]
    return flattened.reshape(groups, out_len, window)


def skew_sum(cross_terms, taps_count):
    groups, block_len, window = cross_terms.shape
    flattened = jnp.pad(cross_terms.reshape(groups, block_len * window), ((0, 0), (0, block_len)))
    return jnp.sum(flattened.reshape(groups, block_len, window + 1)[:, :, :taps_count], axis=1)[
        :, ::-1
    ]


def depthwise(values, kernel):
    channels = values.shape[0]
    return lax.conv_general_dilated(
        values[None],
        kernel[:, None, :],
        window_strides=(1,),
        padding="VALID",
        dimension_numbers=("NCH", "OIH", "NCH"),
        feature_group_count=channels,
        preferred_element_type=jnp.float32,
    )[0]


def banded_kernel(ahead_ref, behind_ref, pw_ref, gw_ref, fo_ref, bo_ref, fg_ref, *, here):
    rows = fo_ref.shape[2]
    lanes = ahead_ref.shape[2]
    dims = (((1,), (1,)), ((), ()))
    flip = (
        lax.broadcasted_iota(jnp.int32, (here, here), 0) + lax.broadcasted_iota(jnp.int32, (here, here), 1)
        == here - 1
    ).astype(jnp.bfloat16)
    for group in range(ahead_ref.shape[0]):
        for row_ref, data_ref, out_ref in ((ahead_ref, pw_ref, fo_ref), (behind_ref, gw_ref, bo_ref)):
            band = pltpu.roll(
                jnp.broadcast_to(row_ref[group], (rows, lanes)), 0, 1, stride=1, stride_axis=0
            ).astype(jnp.bfloat16)
            out_ref[group] = lax.dot_general(
                data_ref[group], band, dims, preferred_element_type=jnp.float32
            )
        gm_rev = jnp.dot(gw_ref[group][:, :here], flip, preferred_element_type=jnp.float32).astype(jnp.bfloat16)
        cross = lax.dot_general(
            gm_rev, pw_ref[group], (((0,), (0,)), ((), ())), preferred_element_type=jnp.float32
        )
        diag = pltpu.roll(cross, lanes - here + 1, 1, stride=1, stride_axis=0)
        fg_ref[group] = jnp.sum(diag, axis=0, keepdims=True)[:, : fg_ref.shape[2]]


def both_convs(product, grad_mixed, filters_low, here):
    channels, win = product.shape
    groups, taps = filters_low.shape
    out_len = win - taps + 1
    rows = -(-out_len // 16) * 16
    lanes = -(-max(win, rows + taps - 1) // 128) * 128
    as_rows = filters_low.astype(jnp.float32)
    ahead = jnp.pad(as_rows[:, ::-1], ((0, 0), (0, lanes - taps))).reshape(groups, 1, lanes)
    behind = jnp.pad(as_rows, ((0, 0), (0, lanes - taps))).reshape(groups, 1, lanes)
    pw = jnp.pad(product, ((0, 0), (0, lanes - win))).reshape(groups, channels // groups, lanes)
    gw = jnp.pad(grad_mixed, ((0, 0), (0, lanes - win))).reshape(groups, channels // groups, lanes)
    step = math.gcd(groups, 4)
    size = channels // groups

    def blocks(*tail):
        return pl.BlockSpec((step,) + tail, lambda i: (i, 0, 0))

    fo, bo, fg = pl.pallas_call(
        functools.partial(banded_kernel, here=here),
        out_shape=(jax.ShapeDtypeStruct((groups, size, rows), jnp.float32),) * 2
        + (jax.ShapeDtypeStruct((groups, 1, taps), jnp.float32),),
        grid=(groups // step,),
        in_specs=[blocks(1, lanes), blocks(1, lanes), blocks(size, lanes), blocks(size, lanes)],
        out_specs=(blocks(size, rows), blocks(size, rows), blocks(1, taps)),
        compiler_params=pltpu.CompilerParams(vmem_limit_bytes=8 * 1024 * 1024),
        cost_estimate=pl.CostEstimate(
            flops=4 * channels * lanes * (rows + here), transcendentals=0, bytes_accessed=4 * channels * (lanes + 2 * rows)
        ),
    )(ahead, behind, pw, gw)
    return fo.reshape(channels, rows)[:, :out_len], bo.reshape(channels, rows)[:, :out_len], fg.reshape(groups, taps)


def shards(outer_gate, inner_gate, value_stream, grad_output, filters, feature_taps, skip_gain):
    channels, block_len = outer_gate.shape
    ctx_size = lax.axis_size("ctx")
    fsdp_size = lax.axis_size("fsdp")
    n_dev = ctx_size * fsdp_size
    groups, taps_here = filters.shape
    taps_count = taps_here * ctx_size
    reach_cols = taps_count - 1
    group_size = channels // groups
    chunk = feature_taps.shape[2]

    row = jnp.concatenate([filters.reshape(-1), feature_taps.reshape(-1), skip_gain])
    gathered = lax.all_to_all(
        jnp.broadcast_to(row[None], (ctx_size, row.shape[0])), "ctx", 0, 0, tiled=True
    )
    n_filt = groups * taps_here
    n_chunk = row.shape[0] - n_filt
    per_block = ctx_size // fsdp_size
    filters_all = (
        gathered[:, :n_filt]
        .reshape(ctx_size, groups, taps_here)
        .transpose(1, 0, 2)
        .reshape(groups, taps_count)
    )
    moved = lax.all_to_all(gathered[:, n_filt:], "fsdp", 0, 0, tiled=True)
    local = (
        moved.reshape(fsdp_size, per_block, n_chunk).transpose(1, 0, 2).reshape(ctx_size, n_chunk)
    )
    taps_all = (
        local[:, : 9 * chunk].reshape(ctx_size, 3, 3, chunk).transpose(1, 2, 0, 3).reshape(3, 3, channels)
    )
    skip_all = local[:, 9 * chunk :].reshape(channels)

    rim = reach_cols + 2
    prev_rim = passed_along(
        jnp.concatenate(
            [outer_gate[:, block_len - 2 :], inner_gate[:, block_len - rim :], value_stream[:, block_len - rim :]],
            axis=1,
        ),
        "ctx",
        1,
    )
    next_rim = passed_along(
        jnp.concatenate(
            [grad_output[:, :rim], outer_gate[:, :rim], inner_gate[:, :2], value_stream[:, :2]], axis=1
        ),
        "ctx",
        -1,
    )
    outer_ext = jnp.concatenate([prev_rim[:, :2], outer_gate, next_rim[:, rim : 2 * rim]], axis=1)
    inner_ext = jnp.concatenate(
        [prev_rim[:, 2 : 2 + rim], inner_gate, next_rim[:, 2 * rim : 2 * rim + 2]], axis=1
    )
    value_ext = jnp.concatenate([prev_rim[:, 2 + rim :], value_stream, next_rim[:, 2 * rim + 2 :]], axis=1)
    upstream = jnp.concatenate([grad_output, next_rim[:, :rim]], axis=1).astype(jnp.float32)

    outer_feat = featurize(outer_ext.astype(jnp.float32), taps_all[0])
    inner_feat = featurize(inner_ext.astype(jnp.float32), taps_all[1])
    value_feat = featurize(value_ext.astype(jnp.float32), taps_all[2])
    product = (inner_feat * value_feat).astype(jnp.bfloat16)

    out_len = block_len + 2
    filters_low = filters_all.astype(jnp.bfloat16)
    product_here = product[:, reach_cols:].astype(jnp.float32)
    grad_mixed = (upstream * outer_feat).astype(jnp.bfloat16)
    convolved, ahead, filter_diag = both_convs(product, grad_mixed, filters_low, block_len)
    mixed = convolved + skip_all[:, None] * product_here
    gated_out = (outer_feat[:, :block_len] * mixed[:, :block_len]).astype(jnp.bfloat16)

    grad_outer_feat = (upstream[:, :out_len] * mixed).astype(jnp.bfloat16)
    grad_product = ahead + skip_all[:, None] * grad_mixed[:, :out_len].astype(jnp.float32)
    grad_inner_feat = (grad_product * value_feat[:, reach_cols:]).astype(jnp.bfloat16)
    grad_value_feat = (grad_product * inner_feat[:, reach_cols:]).astype(jnp.bfloat16)

    grad_outer = carry_back(grad_outer_feat.astype(jnp.float32), taps_all[0])
    grad_inner = carry_back(grad_inner_feat.astype(jnp.float32), taps_all[1])
    grad_value = carry_back(grad_value_feat.astype(jnp.float32), taps_all[2])

    grad_scale = 1.0 / math.sqrt(ctx_size * block_len)
    gm_here = grad_mixed[:, :block_len]
    filter_part = grad_scale * filter_diag[:, ::-1]
    skip_part = grad_scale * jnp.sum(
        gm_here.astype(jnp.float32) * product_here[:, :block_len], axis=1
    )
    taps_part = grad_scale * jnp.stack(
        [
            tap_sums(grad_outer_feat[:, :block_len], outer_ext[:, : block_len + 2]),
            tap_sums(grad_inner_feat[:, :block_len], inner_ext[:, reach_cols : reach_cols + block_len + 2]),
            tap_sums(grad_value_feat[:, :block_len], value_ext[:, reach_cols : reach_cols + block_len + 2]),
        ]
    )

    chunk_parts = jnp.concatenate(
        [
            taps_part.reshape(3, 3, ctx_size, chunk).transpose(2, 0, 1, 3).reshape(ctx_size, -1),
            skip_part.reshape(ctx_size, chunk),
        ],
        axis=1,
    )
    to_fsdp = chunk_parts.reshape(per_block, fsdp_size, n_chunk).transpose(1, 0, 2).reshape(ctx_size, n_chunk)
    by_owner = lax.all_to_all(to_fsdp, "fsdp", 0, 0, tiled=True)
    send = jnp.concatenate(
        [
            filter_part.reshape(groups, ctx_size, taps_here).transpose(1, 0, 2).reshape(ctx_size, -1),
            by_owner,
        ],
        axis=1,
    )
    reduced = jnp.sum(lax.all_to_all(send, "ctx", 0, 0, tiled=True), axis=0)
    filter_share = reduced[:n_filt].reshape(groups, taps_here)
    taps_share = reduced[n_filt : n_filt + 9 * chunk].reshape(3, 3, chunk)
    skip_share = reduced[n_filt + 9 * chunk :]
    return (
        gated_out,
        grad_outer.astype(jnp.bfloat16),
        grad_inner.astype(jnp.bfloat16),
        grad_value.astype(jnp.bfloat16),
        filter_share,
        taps_share,
        skip_share,
    )


def solution(mesh):
    return jax.shard_map(
        shards,
        mesh=mesh,
        in_specs=(
            P("fsdp", "ctx"),
            P("fsdp", "ctx"),
            P("fsdp", "ctx"),
            P("fsdp", "ctx"),
            P("fsdp", "ctx"),
            P(None, None, ("ctx", "fsdp")),
            P(("ctx", "fsdp")),
        ),
        out_specs=(
            P("fsdp", "ctx"),
            P("fsdp", "ctx"),
            P("fsdp", "ctx"),
            P("fsdp", "ctx"),
            P("fsdp", "ctx"),
            P(None, None, ("ctx", "fsdp")),
            P(("ctx", "fsdp")),
        ),
        check_vma=False,
    )
```

```python
import functools
import math

import jax
import jax.numpy as jnp
from jax import lax
from jax.experimental import pallas as pl
from jax.experimental.pallas import tpu as pltpu
from jax.sharding import PartitionSpec as P


def passed_along(shard, axis, by):
    devices = lax.axis_size(axis)
    pairs = [(i, i + by) for i in range(devices) if 0 <= i + by < devices]
    return lax.ppermute(shard, axis, pairs)


def featurize(extended, tap_gains):
    out_len = extended.shape[1] - 2
    result = tap_gains[0][:, None] * extended[:, 2:]
    result = result + tap_gains[1][:, None] * extended[:, 1 : out_len + 1]
    return result + tap_gains[2][:, None] * extended[:, :out_len]


def carry_back(extended, tap_gains):
    out_len = extended.shape[1] - 2
    result = tap_gains[0][:, None] * extended[:, :out_len]
    result = result + tap_gains[1][:, None] * extended[:, 1 : out_len + 1]
    return result + tap_gains[2][:, None] * extended[:, 2:]


def tap_sums(grad_rows, extended):
    block_len = grad_rows.shape[1]
    weighted = grad_rows.astype(jnp.float32)
    return jnp.stack(
        [
            jnp.sum(
                weighted * extended[:, 2 - shift_by : 2 - shift_by + block_len].astype(jnp.float32),
                axis=1,
            )
            for shift_by in range(3)
        ]
    )


def toeplitz_rows(filters_low, out_len):
    groups, taps_count = filters_low.shape
    window = out_len + taps_count - 1
    filter_row = jnp.concatenate(
        [filters_low[:, ::-1], jnp.zeros((groups, window + 1 - taps_count), filters_low.dtype)],
        axis=1,
    )
    flattened = jnp.tile(filter_row, (1, out_len))[:, : out_len * window]
    return flattened.reshape(groups, out_len, window)


def skew_sum(cross_terms, taps_count):
    groups, block_len, window = cross_terms.shape
    flattened = jnp.pad(cross_terms.reshape(groups, block_len * window), ((0, 0), (0, block_len)))
    return jnp.sum(flattened.reshape(groups, block_len, window + 1)[:, :, :taps_count], axis=1)[
        :, ::-1
    ]


def depthwise(values, kernel):
    channels = values.shape[0]
    return lax.conv_general_dilated(
        values[None],
        kernel[:, None, :],
        window_strides=(1,),
        padding="VALID",
        dimension_numbers=("NCH", "OIH", "NCH"),
        feature_group_count=channels,
        preferred_element_type=jnp.float32,
    )[0]


def banded_kernel(ahead_ref, behind_ref, pw_ref, gw_ref, fo_ref, bo_ref, fg_ref, *, here):
    rows = fo_ref.shape[2]
    lanes = ahead_ref.shape[2]
    dims = (((1,), (1,)), ((), ()))
    flip = (
        lax.broadcasted_iota(jnp.int32, (here, here), 0) + lax.broadcasted_iota(jnp.int32, (here, here), 1)
        == here - 1
    ).astype(jnp.bfloat16)
    for group in range(ahead_ref.shape[0]):
        for row_ref, data_ref, out_ref in ((ahead_ref, pw_ref, fo_ref), (behind_ref, gw_ref, bo_ref)):
            band = pltpu.roll(
                jnp.broadcast_to(row_ref[group], (rows, lanes)), 0, 1, stride=1, stride_axis=0
            ).astype(jnp.bfloat16)
            out_ref[group] = lax.dot_general(
                data_ref[group], band, dims, preferred_element_type=jnp.float32
            )
        gm_rev = jnp.dot(gw_ref[group][:, :here], flip, preferred_element_type=jnp.float32).astype(jnp.bfloat16)
        cross = lax.dot_general(
            gm_rev, pw_ref[group], (((0,), (0,)), ((), ())), preferred_element_type=jnp.float32
        )
        diag = pltpu.roll(cross, lanes - here + 1, 1, stride=1, stride_axis=0)
        fg_ref[group] = jnp.sum(diag, axis=0, keepdims=True)[:, : fg_ref.shape[2]]


def both_convs(product, grad_mixed, filters_low, here):
    channels, win = product.shape
    groups, taps = filters_low.shape
    out_len = win - taps + 1
    rows = -(-out_len // 16) * 16
    lanes = -(-max(win, rows + taps - 1) // 128) * 128
    as_rows = filters_low.astype(jnp.float32)
    ahead = jnp.pad(as_rows[:, ::-1], ((0, 0), (0, lanes - taps))).reshape(groups, 1, lanes)
    behind = jnp.pad(as_rows, ((0, 0), (0, lanes - taps))).reshape(groups, 1, lanes)
    pw = jnp.pad(product, ((0, 0), (0, lanes - win))).reshape(groups, channels // groups, lanes)
    gw = jnp.pad(grad_mixed, ((0, 0), (0, lanes - win))).reshape(groups, channels // groups, lanes)
    step = math.gcd(groups, 4)
    size = channels // groups

    def blocks(*tail):
        return pl.BlockSpec((step,) + tail, lambda i: (i, 0, 0))

    fo, bo, fg = pl.pallas_call(
        functools.partial(banded_kernel, here=here),
        out_shape=(jax.ShapeDtypeStruct((groups, size, rows), jnp.float32),) * 2
        + (jax.ShapeDtypeStruct((groups, 1, taps), jnp.float32),),
        grid=(groups // step,),
        in_specs=[blocks(1, lanes), blocks(1, lanes), blocks(size, lanes), blocks(size, lanes)],
        out_specs=(blocks(size, rows), blocks(size, rows), blocks(1, taps)),
        compiler_params=pltpu.CompilerParams(vmem_limit_bytes=8 * 1024 * 1024),
        cost_estimate=pl.CostEstimate(
            flops=4 * channels * lanes * (rows + here), transcendentals=0, bytes_accessed=4 * channels * (lanes + 2 * rows)
        ),
    )(ahead, behind, pw, gw)
    return fo.reshape(channels, rows)[:, :out_len], bo.reshape(channels, rows)[:, :out_len], fg.reshape(groups, taps)


def shards(outer_gate, inner_gate, value_stream, grad_output, filters, feature_taps, skip_gain):
    channels, block_len = outer_gate.shape
    ctx_size = lax.axis_size("ctx")
    fsdp_size = lax.axis_size("fsdp")
    n_dev = ctx_size * fsdp_size
    groups, taps_here = filters.shape
    taps_count = taps_here * ctx_size
    reach_cols = taps_count - 1
    group_size = channels // groups
    chunk = feature_taps.shape[2]

    row = jnp.concatenate([filters.reshape(-1), feature_taps.reshape(-1), skip_gain])
    gathered = lax.all_to_all(
        jnp.broadcast_to(row[None], (ctx_size, row.shape[0])), "ctx", 0, 0, tiled=True
    )
    n_filt = groups * taps_here
    n_chunk = row.shape[0] - n_filt
    per_block = ctx_size // fsdp_size
    filters_all = (
        gathered[:, :n_filt]
        .reshape(ctx_size, groups, taps_here)
        .transpose(1, 0, 2)
        .reshape(groups, taps_count)
    )
    moved = lax.all_to_all(gathered[:, n_filt:], "fsdp", 0, 0, tiled=True)
    local = (
        moved.reshape(fsdp_size, per_block, n_chunk).transpose(1, 0, 2).reshape(ctx_size, n_chunk)
    )
    taps_all = (
        local[:, : 9 * chunk].reshape(ctx_size, 3, 3, chunk).transpose(1, 2, 0, 3).reshape(3, 3, channels)
    )
    skip_all = local[:, 9 * chunk :].reshape(channels)

    rim = reach_cols + 2
    prev_rim = passed_along(
        jnp.concatenate(
            [outer_gate[:, block_len - 2 :], inner_gate[:, block_len - rim :], value_stream[:, block_len - rim :]],
            axis=1,
        ),
        "ctx",
        1,
    )
    next_rim = passed_along(
        jnp.concatenate(
            [grad_output[:, :rim], outer_gate[:, :rim], inner_gate[:, :2], value_stream[:, :2]], axis=1
        ),
        "ctx",
        -1,
    )
    outer_ext = jnp.concatenate([prev_rim[:, :2], outer_gate, next_rim[:, rim : 2 * rim]], axis=1)
    inner_ext = jnp.concatenate(
        [prev_rim[:, 2 : 2 + rim], inner_gate, next_rim[:, 2 * rim : 2 * rim + 2]], axis=1
    )
    value_ext = jnp.concatenate([prev_rim[:, 2 + rim :], value_stream, next_rim[:, 2 * rim + 2 :]], axis=1)
    upstream = jnp.concatenate([grad_output, next_rim[:, :rim]], axis=1).astype(jnp.float32)

    outer_feat = featurize(outer_ext.astype(jnp.float32), taps_all[0])
    inner_feat = featurize(inner_ext.astype(jnp.float32), taps_all[1])
    value_feat = featurize(value_ext.astype(jnp.float32), taps_all[2])
    product = (inner_feat * value_feat).astype(jnp.bfloat16)

    out_len = block_len + 2
    filters_low = filters_all.astype(jnp.bfloat16)
    product_here = product[:, reach_cols:].astype(jnp.float32)
    grad_mixed = (upstream * outer_feat).astype(jnp.bfloat16)
    convolved, ahead, filter_diag = both_convs(product, grad_mixed, filters_low, block_len)
    mixed = convolved + skip_all[:, None] * product_here

    grad_outer_feat = (upstream[:, :out_len] * mixed).astype(jnp.bfloat16)
    grad_product = ahead + skip_all[:, None] * grad_mixed[:, :out_len].astype(jnp.float32)
    grad_inner_feat = (grad_product * value_feat[:, reach_cols:]).astype(jnp.bfloat16)
    grad_value_feat = (grad_product * inner_feat[:, reach_cols:]).astype(jnp.bfloat16)

    grad_scale = 1.0 / math.sqrt(ctx_size * block_len)
    gm_here = grad_mixed[:, :block_len]
    filter_part = grad_scale * filter_diag[:, ::-1]
    skip_part = grad_scale * jnp.sum(
        gm_here.astype(jnp.float32) * product_here[:, :block_len], axis=1
    )
    taps_part = grad_scale * jnp.stack(
        [
            tap_sums(grad_outer_feat[:, :block_len], outer_ext[:, : block_len + 2]),
            tap_sums(grad_inner_feat[:, :block_len], inner_ext[:, reach_cols : reach_cols + block_len + 2]),
            tap_sums(grad_value_feat[:, :block_len], value_ext[:, reach_cols : reach_cols + block_len + 2]),
        ]
    )

    chunk_parts = jnp.concatenate(
        [
            taps_part.reshape(3, 3, ctx_size, chunk).transpose(2, 0, 1, 3).reshape(ctx_size, -1),
            skip_part.reshape(ctx_size, chunk),
        ],
        axis=1,
    )
    to_fsdp = chunk_parts.reshape(per_block, fsdp_size, n_chunk).transpose(1, 0, 2).reshape(ctx_size, n_chunk)
    by_owner = lax.all_to_all(to_fsdp, "fsdp", 0, 0, tiled=True)
    by_owner, outer_feat, mixed, grad_outer_feat, grad_inner_feat, grad_value_feat = lax.optimization_barrier(
        (by_owner, outer_feat, mixed, grad_outer_feat, grad_inner_feat, grad_value_feat)
    )
    gated_out = (outer_feat[:, :block_len] * mixed[:, :block_len]).astype(jnp.bfloat16)
    grad_outer = carry_back(grad_outer_feat.astype(jnp.float32), taps_all[0])
    grad_inner = carry_back(grad_inner_feat.astype(jnp.float32), taps_all[1])
    grad_value = carry_back(grad_value_feat.astype(jnp.float32), taps_all[2])

    send = jnp.concatenate(
        [
            filter_part.reshape(groups, ctx_size, taps_here).transpose(1, 0, 2).reshape(ctx_size, -1),
            by_owner,
        ],
        axis=1,
    )
    reduced = jnp.sum(lax.all_to_all(send, "ctx", 0, 0, tiled=True), axis=0)
    filter_share = reduced[:n_filt].reshape(groups, taps_here)
    taps_share = reduced[n_filt : n_filt + 9 * chunk].reshape(3, 3, chunk)
    skip_share = reduced[n_filt + 9 * chunk :]
    return (
        gated_out,
        grad_outer.astype(jnp.bfloat16),
        grad_inner.astype(jnp.bfloat16),
        grad_value.astype(jnp.bfloat16),
        filter_share,
        taps_share,
        skip_share,
    )


def solution(mesh):
    return jax.shard_map(
        shards,
        mesh=mesh,
        in_specs=(
            P("fsdp", "ctx"),
            P("fsdp", "ctx"),
            P("fsdp", "ctx"),
            P("fsdp", "ctx"),
            P("fsdp", "ctx"),
            P(None, None, ("ctx", "fsdp")),
            P(("ctx", "fsdp")),
        ),
        out_specs=(
            P("fsdp", "ctx"),
            P("fsdp", "ctx"),
            P("fsdp", "ctx"),
            P("fsdp", "ctx"),
            P("fsdp", "ctx"),
            P(None, None, ("ctx", "fsdp")),
            P(("ctx", "fsdp")),
        ),
        check_vma=False,
    )
```

```python
import functools
import math

import jax
import jax.numpy as jnp
from jax import lax
from jax.experimental import pallas as pl
from jax.experimental.pallas import tpu as pltpu
from jax.sharding import PartitionSpec as P


def passed_along(shard, axis, by):
    devices = lax.axis_size(axis)
    pairs = [(i, i + by) for i in range(devices) if 0 <= i + by < devices]
    return lax.ppermute(shard, axis, pairs)


def featurize(extended, tap_gains):
    out_len = extended.shape[1] - 2
    result = tap_gains[0][:, None] * extended[:, 2:]
    result = result + tap_gains[1][:, None] * extended[:, 1 : out_len + 1]
    return result + tap_gains[2][:, None] * extended[:, :out_len]


def carry_back(extended, tap_gains):
    out_len = extended.shape[1] - 2
    result = tap_gains[0][:, None] * extended[:, :out_len]
    result = result + tap_gains[1][:, None] * extended[:, 1 : out_len + 1]
    return result + tap_gains[2][:, None] * extended[:, 2:]


def tap_sums(grad_rows, extended):
    block_len = grad_rows.shape[1]
    weighted = grad_rows.astype(jnp.float32)
    return jnp.stack(
        [
            jnp.sum(
                weighted * extended[:, 2 - shift_by : 2 - shift_by + block_len].astype(jnp.float32),
                axis=1,
            )
            for shift_by in range(3)
        ]
    )


def toeplitz_rows(filters_low, out_len):
    groups, taps_count = filters_low.shape
    window = out_len + taps_count - 1
    filter_row = jnp.concatenate(
        [filters_low[:, ::-1], jnp.zeros((groups, window + 1 - taps_count), filters_low.dtype)],
        axis=1,
    )
    flattened = jnp.tile(filter_row, (1, out_len))[:, : out_len * window]
    return flattened.reshape(groups, out_len, window)


def skew_sum(cross_terms, taps_count):
    groups, block_len, window = cross_terms.shape
    flattened = jnp.pad(cross_terms.reshape(groups, block_len * window), ((0, 0), (0, block_len)))
    return jnp.sum(flattened.reshape(groups, block_len, window + 1)[:, :, :taps_count], axis=1)[
        :, ::-1
    ]


def depthwise(values, kernel):
    channels = values.shape[0]
    return lax.conv_general_dilated(
        values[None],
        kernel[:, None, :],
        window_strides=(1,),
        padding="VALID",
        dimension_numbers=("NCH", "OIH", "NCH"),
        feature_group_count=channels,
        preferred_element_type=jnp.float32,
    )[0]


def banded_kernel(ahead_ref, behind_ref, pw_ref, gw_ref, fo_ref, bo_ref, fg_ref, *, here):
    rows = fo_ref.shape[2]
    lanes = ahead_ref.shape[2]
    dims = (((1,), (1,)), ((), ()))
    flip = (
        lax.broadcasted_iota(jnp.int32, (here, here), 0) + lax.broadcasted_iota(jnp.int32, (here, here), 1)
        == here - 1
    ).astype(jnp.bfloat16)
    for group in range(ahead_ref.shape[0]):
        for row_ref, data_ref, out_ref in ((ahead_ref, pw_ref, fo_ref), (behind_ref, gw_ref, bo_ref)):
            band = pltpu.roll(
                jnp.broadcast_to(row_ref[group], (rows, lanes)), 0, 1, stride=1, stride_axis=0
            ).astype(jnp.bfloat16)
            out_ref[group] = lax.dot_general(
                data_ref[group], band, dims, preferred_element_type=jnp.float32
            )
        gm_rev = jnp.dot(gw_ref[group][:, :here], flip, preferred_element_type=jnp.float32).astype(jnp.bfloat16)
        cross = lax.dot_general(
            gm_rev, pw_ref[group], (((0,), (0,)), ((), ())), preferred_element_type=jnp.float32
        )
        diag = pltpu.roll(cross, lanes - here + 1, 1, stride=1, stride_axis=0)
        fg_ref[group] = jnp.sum(diag, axis=0, keepdims=True)[:, : fg_ref.shape[2]]


def both_convs(product, grad_mixed, filters_low, here):
    channels, win = product.shape
    groups, taps = filters_low.shape
    out_len = win - taps + 1
    rows = -(-out_len // 16) * 16
    lanes = -(-max(win, rows + taps - 1) // 128) * 128
    as_rows = filters_low.astype(jnp.float32)
    ahead = jnp.pad(as_rows[:, ::-1], ((0, 0), (0, lanes - taps))).reshape(groups, 1, lanes)
    behind = jnp.pad(as_rows, ((0, 0), (0, lanes - taps))).reshape(groups, 1, lanes)
    pw = jnp.pad(product, ((0, 0), (0, lanes - win))).reshape(groups, channels // groups, lanes)
    gw = jnp.pad(grad_mixed, ((0, 0), (0, lanes - win))).reshape(groups, channels // groups, lanes)
    step = math.gcd(groups, 4)
    size = channels // groups

    def blocks(*tail):
        return pl.BlockSpec((step,) + tail, lambda i: (i, 0, 0))

    fo, bo, fg = pl.pallas_call(
        functools.partial(banded_kernel, here=here),
        out_shape=(jax.ShapeDtypeStruct((groups, size, rows), jnp.float32),) * 2
        + (jax.ShapeDtypeStruct((groups, 1, taps), jnp.float32),),
        grid=(groups // step,),
        in_specs=[blocks(1, lanes), blocks(1, lanes), blocks(size, lanes), blocks(size, lanes)],
        out_specs=(blocks(size, rows), blocks(size, rows), blocks(1, taps)),
        compiler_params=pltpu.CompilerParams(vmem_limit_bytes=8 * 1024 * 1024),
        cost_estimate=pl.CostEstimate(
            flops=4 * channels * lanes * (rows + here), transcendentals=0, bytes_accessed=4 * channels * (lanes + 2 * rows)
        ),
    )(ahead, behind, pw, gw)
    return fo.reshape(channels, rows)[:, :out_len], bo.reshape(channels, rows)[:, :out_len], fg.reshape(groups, taps)


def shards(outer_gate, inner_gate, value_stream, grad_output, filters, feature_taps, skip_gain):
    channels, block_len = outer_gate.shape
    ctx_size = lax.axis_size("ctx")
    fsdp_size = lax.axis_size("fsdp")
    n_dev = ctx_size * fsdp_size
    groups, taps_here = filters.shape
    taps_count = taps_here * ctx_size
    reach_cols = taps_count - 1
    group_size = channels // groups
    chunk = feature_taps.shape[2]

    rim = reach_cols + 2
    prev_rim = passed_along(
        jnp.concatenate(
            [outer_gate[:, block_len - 2 :], inner_gate[:, block_len - rim :], value_stream[:, block_len - rim :]],
            axis=1,
        ),
        "ctx",
        1,
    )
    next_rim = passed_along(
        jnp.concatenate(
            [grad_output[:, :rim], outer_gate[:, :rim], inner_gate[:, :2], value_stream[:, :2]], axis=1
        ),
        "ctx",
        -1,
    )
    row = jnp.concatenate([filters.reshape(-1), feature_taps.reshape(-1), skip_gain])
    row, prev_rim, next_rim = lax.optimization_barrier((row, prev_rim, next_rim))
    gathered = lax.all_to_all(
        jnp.broadcast_to(row[None], (ctx_size, row.shape[0])), "ctx", 0, 0, tiled=True
    )
    n_filt = groups * taps_here
    n_chunk = row.shape[0] - n_filt
    per_block = ctx_size // fsdp_size
    filters_all = (
        gathered[:, :n_filt]
        .reshape(ctx_size, groups, taps_here)
        .transpose(1, 0, 2)
        .reshape(groups, taps_count)
    )
    moved = lax.all_to_all(gathered[:, n_filt:], "fsdp", 0, 0, tiled=True)
    local = (
        moved.reshape(fsdp_size, per_block, n_chunk).transpose(1, 0, 2).reshape(ctx_size, n_chunk)
    )
    taps_all = (
        local[:, : 9 * chunk].reshape(ctx_size, 3, 3, chunk).transpose(1, 2, 0, 3).reshape(3, 3, channels)
    )
    skip_all = local[:, 9 * chunk :].reshape(channels)

    outer_ext = jnp.concatenate([prev_rim[:, :2], outer_gate, next_rim[:, rim : 2 * rim]], axis=1)
    inner_ext = jnp.concatenate(
        [prev_rim[:, 2 : 2 + rim], inner_gate, next_rim[:, 2 * rim : 2 * rim + 2]], axis=1
    )
    value_ext = jnp.concatenate([prev_rim[:, 2 + rim :], value_stream, next_rim[:, 2 * rim + 2 :]], axis=1)
    upstream = jnp.concatenate([grad_output, next_rim[:, :rim]], axis=1).astype(jnp.float32)

    outer_feat = featurize(outer_ext.astype(jnp.float32), taps_all[0])
    inner_feat = featurize(inner_ext.astype(jnp.float32), taps_all[1])
    value_feat = featurize(value_ext.astype(jnp.float32), taps_all[2])
    product = (inner_feat * value_feat).astype(jnp.bfloat16)

    out_len = block_len + 2
    filters_low = filters_all.astype(jnp.bfloat16)
    product_here = product[:, reach_cols:].astype(jnp.float32)
    grad_mixed = (upstream * outer_feat).astype(jnp.bfloat16)
    convolved, ahead, filter_diag = both_convs(product, grad_mixed, filters_low, block_len)
    mixed = convolved + skip_all[:, None] * product_here

    grad_outer_feat = (upstream[:, :out_len] * mixed).astype(jnp.bfloat16)
    grad_product = ahead + skip_all[:, None] * grad_mixed[:, :out_len].astype(jnp.float32)
    grad_inner_feat = (grad_product * value_feat[:, reach_cols:]).astype(jnp.bfloat16)
    grad_value_feat = (grad_product * inner_feat[:, reach_cols:]).astype(jnp.bfloat16)

    grad_scale = 1.0 / math.sqrt(ctx_size * block_len)
    gm_here = grad_mixed[:, :block_len]
    filter_part = grad_scale * filter_diag[:, ::-1]
    skip_part = grad_scale * jnp.sum(
        gm_here.astype(jnp.float32) * product_here[:, :block_len], axis=1
    )
    taps_part = grad_scale * jnp.stack(
        [
            tap_sums(grad_outer_feat[:, :block_len], outer_ext[:, : block_len + 2]),
            tap_sums(grad_inner_feat[:, :block_len], inner_ext[:, reach_cols : reach_cols + block_len + 2]),
            tap_sums(grad_value_feat[:, :block_len], value_ext[:, reach_cols : reach_cols + block_len + 2]),
        ]
    )

    chunk_parts = jnp.concatenate(
        [
            taps_part.reshape(3, 3, ctx_size, chunk).transpose(2, 0, 1, 3).reshape(ctx_size, -1),
            skip_part.reshape(ctx_size, chunk),
        ],
        axis=1,
    )
    to_fsdp = chunk_parts.reshape(per_block, fsdp_size, n_chunk).transpose(1, 0, 2).reshape(ctx_size, n_chunk)
    by_owner = lax.all_to_all(to_fsdp, "fsdp", 0, 0, tiled=True)
    by_owner, outer_feat, mixed, grad_outer_feat, grad_inner_feat, grad_value_feat = lax.optimization_barrier(
        (by_owner, outer_feat, mixed, grad_outer_feat, grad_inner_feat, grad_value_feat)
    )
    gated_out = (outer_feat[:, :block_len] * mixed[:, :block_len]).astype(jnp.bfloat16)
    grad_outer = carry_back(grad_outer_feat.astype(jnp.float32), taps_all[0])
    grad_inner = carry_back(grad_inner_feat.astype(jnp.float32), taps_all[1])
    grad_value = carry_back(grad_value_feat.astype(jnp.float32), taps_all[2])

    send = jnp.concatenate(
        [
            filter_part.reshape(groups, ctx_size, taps_here).transpose(1, 0, 2).reshape(ctx_size, -1),
            by_owner,
        ],
        axis=1,
    )
    reduced = jnp.sum(lax.all_to_all(send, "ctx", 0, 0, tiled=True), axis=0)
    filter_share = reduced[:n_filt].reshape(groups, taps_here)
    taps_share = reduced[n_filt : n_filt + 9 * chunk].reshape(3, 3, chunk)
    skip_share = reduced[n_filt + 9 * chunk :]
    return (
        gated_out,
        grad_outer.astype(jnp.bfloat16),
        grad_inner.astype(jnp.bfloat16),
        grad_value.astype(jnp.bfloat16),
        filter_share,
        taps_share,
        skip_share,
    )


def solution(mesh):
    return jax.shard_map(
        shards,
        mesh=mesh,
        in_specs=(
            P("fsdp", "ctx"),
            P("fsdp", "ctx"),
            P("fsdp", "ctx"),
            P("fsdp", "ctx"),
            P("fsdp", "ctx"),
            P(None, None, ("ctx", "fsdp")),
            P(("ctx", "fsdp")),
        ),
        out_specs=(
            P("fsdp", "ctx"),
            P("fsdp", "ctx"),
            P("fsdp", "ctx"),
            P("fsdp", "ctx"),
            P("fsdp", "ctx"),
            P(None, None, ("ctx", "fsdp")),
            P(("ctx", "fsdp")),
        ),
        check_vma=False,
    )
```

```python
import functools
import math

import jax
import jax.numpy as jnp
from jax import lax
from jax.experimental import pallas as pl
from jax.experimental.pallas import tpu as pltpu
from jax.sharding import PartitionSpec as P


def passed_along(shard, axis, by):
    devices = lax.axis_size(axis)
    pairs = [(i, i + by) for i in range(devices) if 0 <= i + by < devices]
    return lax.ppermute(shard, axis, pairs)


def featurize(extended, tap_gains):
    out_len = extended.shape[1] - 2
    result = tap_gains[0][:, None] * extended[:, 2:]
    result = result + tap_gains[1][:, None] * extended[:, 1 : out_len + 1]
    return result + tap_gains[2][:, None] * extended[:, :out_len]


def carry_back(extended, tap_gains):
    out_len = extended.shape[1] - 2
    result = tap_gains[0][:, None] * extended[:, :out_len]
    result = result + tap_gains[1][:, None] * extended[:, 1 : out_len + 1]
    return result + tap_gains[2][:, None] * extended[:, 2:]


def tap_sums(grad_rows, extended):
    block_len = grad_rows.shape[1]
    weighted = grad_rows.astype(jnp.float32)
    return jnp.stack(
        [
            jnp.sum(
                weighted * extended[:, 2 - shift_by : 2 - shift_by + block_len].astype(jnp.float32),
                axis=1,
            )
            for shift_by in range(3)
        ]
    )


def toeplitz_rows(filters_low, out_len):
    groups, taps_count = filters_low.shape
    window = out_len + taps_count - 1
    filter_row = jnp.concatenate(
        [filters_low[:, ::-1], jnp.zeros((groups, window + 1 - taps_count), filters_low.dtype)],
        axis=1,
    )
    flattened = jnp.tile(filter_row, (1, out_len))[:, : out_len * window]
    return flattened.reshape(groups, out_len, window)


def skew_sum(cross_terms, taps_count):
    groups, block_len, window = cross_terms.shape
    flattened = jnp.pad(cross_terms.reshape(groups, block_len * window), ((0, 0), (0, block_len)))
    return jnp.sum(flattened.reshape(groups, block_len, window + 1)[:, :, :taps_count], axis=1)[
        :, ::-1
    ]


def depthwise(values, kernel):
    channels = values.shape[0]
    return lax.conv_general_dilated(
        values[None],
        kernel[:, None, :],
        window_strides=(1,),
        padding="VALID",
        dimension_numbers=("NCH", "OIH", "NCH"),
        feature_group_count=channels,
        preferred_element_type=jnp.float32,
    )[0]


def banded_kernel(ahead_ref, behind_ref, pw_ref, gw_ref, fo_ref, bo_ref, fg_ref, *, here):
    rows = fo_ref.shape[2]
    lanes = ahead_ref.shape[2]
    dims = (((1,), (1,)), ((), ()))
    flip = (
        lax.broadcasted_iota(jnp.int32, (here, here), 0) + lax.broadcasted_iota(jnp.int32, (here, here), 1)
        == here - 1
    ).astype(jnp.bfloat16)
    for group in range(ahead_ref.shape[0]):
        for row_ref, data_ref, out_ref in ((ahead_ref, pw_ref, fo_ref), (behind_ref, gw_ref, bo_ref)):
            band = pltpu.roll(
                jnp.broadcast_to(row_ref[group], (rows, lanes)), 0, 1, stride=1, stride_axis=0
            ).astype(jnp.bfloat16)
            out_ref[group] = lax.dot_general(
                data_ref[group], band, dims, preferred_element_type=jnp.float32
            )
        gm_rev = jnp.dot(gw_ref[group][:, :here], flip, preferred_element_type=jnp.float32).astype(jnp.bfloat16)
        cross = lax.dot_general(
            gm_rev, pw_ref[group], (((0,), (0,)), ((), ())), preferred_element_type=jnp.float32
        )
        diag = pltpu.roll(cross, lanes - here + 1, 1, stride=1, stride_axis=0)
        fg_ref[group] = jnp.sum(diag, axis=0, keepdims=True)[:, : fg_ref.shape[2]]


def both_convs(product, grad_mixed, filters_low, here):
    channels, win = product.shape
    groups, taps = filters_low.shape
    out_len = win - taps + 1
    rows = -(-out_len // 16) * 16
    lanes = -(-max(win, rows + taps - 1) // 128) * 128
    as_rows = filters_low.astype(jnp.float32)
    ahead = jnp.pad(as_rows[:, ::-1], ((0, 0), (0, lanes - taps))).reshape(groups, 1, lanes)
    behind = jnp.pad(as_rows, ((0, 0), (0, lanes - taps))).reshape(groups, 1, lanes)
    pw = jnp.pad(product, ((0, 0), (0, lanes - win))).reshape(groups, channels // groups, lanes)
    gw = jnp.pad(grad_mixed, ((0, 0), (0, lanes - win))).reshape(groups, channels // groups, lanes)
    step = math.gcd(groups, 4)
    size = channels // groups

    def blocks(*tail):
        return pl.BlockSpec((step,) + tail, lambda i: (i, 0, 0))

    fo, bo, fg = pl.pallas_call(
        functools.partial(banded_kernel, here=here),
        out_shape=(jax.ShapeDtypeStruct((groups, size, rows), jnp.float32),) * 2
        + (jax.ShapeDtypeStruct((groups, 1, taps), jnp.float32),),
        grid=(groups // step,),
        in_specs=[blocks(1, lanes), blocks(1, lanes), blocks(size, lanes), blocks(size, lanes)],
        out_specs=(blocks(size, rows), blocks(size, rows), blocks(1, taps)),
        compiler_params=pltpu.CompilerParams(vmem_limit_bytes=8 * 1024 * 1024),
        cost_estimate=pl.CostEstimate(
            flops=4 * channels * lanes * (rows + here), transcendentals=0, bytes_accessed=4 * channels * (lanes + 2 * rows)
        ),
    )(ahead, behind, pw, gw)
    return fo.reshape(channels, rows)[:, :out_len], bo.reshape(channels, rows)[:, :out_len], fg.reshape(groups, taps)


def shards(outer_gate, inner_gate, value_stream, grad_output, filters, feature_taps, skip_gain):
    channels, block_len = outer_gate.shape
    ctx_size = lax.axis_size("ctx")
    fsdp_size = lax.axis_size("fsdp")
    n_dev = ctx_size * fsdp_size
    groups, taps_here = filters.shape
    taps_count = taps_here * ctx_size
    reach_cols = taps_count - 1
    group_size = channels // groups
    chunk = feature_taps.shape[2]

    pack = jnp.concatenate([feature_taps.reshape(-1), skip_gain])
    n_chunk = pack.shape[0]
    ring = lax.all_to_all(jnp.broadcast_to(pack[None], (fsdp_size, n_chunk)), "fsdp", 0, 0, tiled=True)
    row = jnp.concatenate([filters.reshape(-1), ring.reshape(-1)])
    gathered = lax.all_to_all(
        jnp.broadcast_to(row[None], (ctx_size, row.shape[0])), "ctx", 0, 0, tiled=True
    )
    n_filt = groups * taps_here
    per_block = ctx_size // fsdp_size
    filters_all = (
        gathered[:, :n_filt]
        .reshape(ctx_size, groups, taps_here)
        .transpose(1, 0, 2)
        .reshape(groups, taps_count)
    )
    local = lax.dynamic_slice_in_dim(
        gathered[:, n_filt:], lax.axis_index("fsdp") * per_block, per_block, 0
    ).reshape(ctx_size, n_chunk)
    taps_all = (
        local[:, : 9 * chunk].reshape(ctx_size, 3, 3, chunk).transpose(1, 2, 0, 3).reshape(3, 3, channels)
    )
    skip_all = local[:, 9 * chunk :].reshape(channels)

    rim = reach_cols + 2
    prev_rim = passed_along(
        jnp.concatenate(
            [outer_gate[:, block_len - 2 :], inner_gate[:, block_len - rim :], value_stream[:, block_len - rim :]],
            axis=1,
        ),
        "ctx",
        1,
    )
    next_rim = passed_along(
        jnp.concatenate(
            [grad_output[:, :rim], outer_gate[:, :rim], inner_gate[:, :2], value_stream[:, :2]], axis=1
        ),
        "ctx",
        -1,
    )
    outer_ext = jnp.concatenate([prev_rim[:, :2], outer_gate, next_rim[:, rim : 2 * rim]], axis=1)
    inner_ext = jnp.concatenate(
        [prev_rim[:, 2 : 2 + rim], inner_gate, next_rim[:, 2 * rim : 2 * rim + 2]], axis=1
    )
    value_ext = jnp.concatenate([prev_rim[:, 2 + rim :], value_stream, next_rim[:, 2 * rim + 2 :]], axis=1)
    upstream = jnp.concatenate([grad_output, next_rim[:, :rim]], axis=1).astype(jnp.float32)

    outer_feat = featurize(outer_ext.astype(jnp.float32), taps_all[0])
    inner_feat = featurize(inner_ext.astype(jnp.float32), taps_all[1])
    value_feat = featurize(value_ext.astype(jnp.float32), taps_all[2])
    product = (inner_feat * value_feat).astype(jnp.bfloat16)

    out_len = block_len + 2
    filters_low = filters_all.astype(jnp.bfloat16)
    product_here = product[:, reach_cols:].astype(jnp.float32)
    grad_mixed = (upstream * outer_feat).astype(jnp.bfloat16)
    convolved, ahead, filter_diag = both_convs(product, grad_mixed, filters_low, block_len)
    mixed = convolved + skip_all[:, None] * product_here

    grad_outer_feat = (upstream[:, :out_len] * mixed).astype(jnp.bfloat16)
    grad_product = ahead + skip_all[:, None] * grad_mixed[:, :out_len].astype(jnp.float32)
    grad_inner_feat = (grad_product * value_feat[:, reach_cols:]).astype(jnp.bfloat16)
    grad_value_feat = (grad_product * inner_feat[:, reach_cols:]).astype(jnp.bfloat16)

    grad_scale = 1.0 / math.sqrt(ctx_size * block_len)
    gm_here = grad_mixed[:, :block_len]
    filter_part = grad_scale * filter_diag[:, ::-1]
    skip_part = grad_scale * jnp.sum(
        gm_here.astype(jnp.float32) * product_here[:, :block_len], axis=1
    )
    taps_part = grad_scale * jnp.stack(
        [
            tap_sums(grad_outer_feat[:, :block_len], outer_ext[:, : block_len + 2]),
            tap_sums(grad_inner_feat[:, :block_len], inner_ext[:, reach_cols : reach_cols + block_len + 2]),
            tap_sums(grad_value_feat[:, :block_len], value_ext[:, reach_cols : reach_cols + block_len + 2]),
        ]
    )

    chunk_parts = jnp.concatenate(
        [
            taps_part.reshape(3, 3, ctx_size, chunk).transpose(2, 0, 1, 3).reshape(ctx_size, -1),
            skip_part.reshape(ctx_size, chunk),
        ],
        axis=1,
    )
    to_fsdp = chunk_parts.reshape(per_block, fsdp_size, n_chunk).transpose(1, 0, 2).reshape(ctx_size, n_chunk)
    by_owner = lax.all_to_all(to_fsdp, "fsdp", 0, 0, tiled=True)
    by_owner, outer_feat, mixed, grad_outer_feat, grad_inner_feat, grad_value_feat = lax.optimization_barrier(
        (by_owner, outer_feat, mixed, grad_outer_feat, grad_inner_feat, grad_value_feat)
    )
    gated_out = (outer_feat[:, :block_len] * mixed[:, :block_len]).astype(jnp.bfloat16)
    grad_outer = carry_back(grad_outer_feat.astype(jnp.float32), taps_all[0])
    grad_inner = carry_back(grad_inner_feat.astype(jnp.float32), taps_all[1])
    grad_value = carry_back(grad_value_feat.astype(jnp.float32), taps_all[2])

    send = jnp.concatenate(
        [
            filter_part.reshape(groups, ctx_size, taps_here).transpose(1, 0, 2).reshape(ctx_size, -1),
            by_owner,
        ],
        axis=1,
    )
    reduced = jnp.sum(lax.all_to_all(send, "ctx", 0, 0, tiled=True), axis=0)
    filter_share = reduced[:n_filt].reshape(groups, taps_here)
    taps_share = reduced[n_filt : n_filt + 9 * chunk].reshape(3, 3, chunk)
    skip_share = reduced[n_filt + 9 * chunk :]
    return (
        gated_out,
        grad_outer.astype(jnp.bfloat16),
        grad_inner.astype(jnp.bfloat16),
        grad_value.astype(jnp.bfloat16),
        filter_share,
        taps_share,
        skip_share,
    )


def solution(mesh):
    return jax.shard_map(
        shards,
        mesh=mesh,
        in_specs=(
            P("fsdp", "ctx"),
            P("fsdp", "ctx"),
            P("fsdp", "ctx"),
            P("fsdp", "ctx"),
            P("fsdp", "ctx"),
            P(None, None, ("ctx", "fsdp")),
            P(("ctx", "fsdp")),
        ),
        out_specs=(
            P("fsdp", "ctx"),
            P("fsdp", "ctx"),
            P("fsdp", "ctx"),
            P("fsdp", "ctx"),
            P("fsdp", "ctx"),
            P(None, None, ("ctx", "fsdp")),
            P(("ctx", "fsdp")),
        ),
        check_vma=False,
    )
```

```python
import functools
import math

import jax
import jax.numpy as jnp
from jax import lax
from jax.experimental import pallas as pl
from jax.experimental.pallas import tpu as pltpu
from jax.sharding import PartitionSpec as P


def passed_along(shard, axis, by):
    devices = lax.axis_size(axis)
    pairs = [(i, i + by) for i in range(devices) if 0 <= i + by < devices]
    return lax.ppermute(shard, axis, pairs)


def featurize(extended, tap_gains):
    out_len = extended.shape[1] - 2
    result = tap_gains[0][:, None] * extended[:, 2:]
    result = result + tap_gains[1][:, None] * extended[:, 1 : out_len + 1]
    return result + tap_gains[2][:, None] * extended[:, :out_len]


def carry_back(extended, tap_gains):
    out_len = extended.shape[1] - 2
    result = tap_gains[0][:, None] * extended[:, :out_len]
    result = result + tap_gains[1][:, None] * extended[:, 1 : out_len + 1]
    return result + tap_gains[2][:, None] * extended[:, 2:]


def tap_sums(grad_rows, extended):
    block_len = grad_rows.shape[1]
    weighted = grad_rows.astype(jnp.float32)
    return jnp.stack(
        [
            jnp.sum(
                weighted * extended[:, 2 - shift_by : 2 - shift_by + block_len].astype(jnp.float32),
                axis=1,
            )
            for shift_by in range(3)
        ]
    )


def toeplitz_rows(filters_low, out_len):
    groups, taps_count = filters_low.shape
    window = out_len + taps_count - 1
    filter_row = jnp.concatenate(
        [filters_low[:, ::-1], jnp.zeros((groups, window + 1 - taps_count), filters_low.dtype)],
        axis=1,
    )
    flattened = jnp.tile(filter_row, (1, out_len))[:, : out_len * window]
    return flattened.reshape(groups, out_len, window)


def skew_sum(cross_terms, taps_count):
    groups, block_len, window = cross_terms.shape
    flattened = jnp.pad(cross_terms.reshape(groups, block_len * window), ((0, 0), (0, block_len)))
    return jnp.sum(flattened.reshape(groups, block_len, window + 1)[:, :, :taps_count], axis=1)[
        :, ::-1
    ]


def depthwise(values, kernel):
    channels = values.shape[0]
    return lax.conv_general_dilated(
        values[None],
        kernel[:, None, :],
        window_strides=(1,),
        padding="VALID",
        dimension_numbers=("NCH", "OIH", "NCH"),
        feature_group_count=channels,
        preferred_element_type=jnp.float32,
    )[0]


def banded_kernel(ahead_ref, behind_ref, pw_ref, gw_ref, fo_ref, bo_ref, fg_ref, *, here):
    rows = fo_ref.shape[2]
    lanes = ahead_ref.shape[2]
    dims = (((1,), (1,)), ((), ()))
    flip = (
        lax.broadcasted_iota(jnp.int32, (here, here), 0) + lax.broadcasted_iota(jnp.int32, (here, here), 1)
        == here - 1
    ).astype(jnp.bfloat16)
    for group in range(ahead_ref.shape[0]):
        for row_ref, data_ref, out_ref in ((ahead_ref, pw_ref, fo_ref), (behind_ref, gw_ref, bo_ref)):
            band = pltpu.roll(
                jnp.broadcast_to(row_ref[group], (rows, lanes)), 0, 1, stride=1, stride_axis=0
            ).astype(jnp.bfloat16)
            out_ref[group] = lax.dot_general(
                data_ref[group], band, dims, preferred_element_type=jnp.float32
            )
        gm_rev = jnp.dot(gw_ref[group][:, :here], flip, preferred_element_type=jnp.float32).astype(jnp.bfloat16)
        cross = lax.dot_general(
            gm_rev, pw_ref[group], (((0,), (0,)), ((), ())), preferred_element_type=jnp.float32
        )
        diag = pltpu.roll(cross, lanes - here + 1, 1, stride=1, stride_axis=0)
        fg_ref[group] = jnp.sum(diag, axis=0, keepdims=True)[:, : fg_ref.shape[2]]


def both_convs(product, grad_mixed, filters_low, here):
    channels, win = product.shape
    groups, taps = filters_low.shape
    out_len = win - taps + 1
    rows = -(-out_len // 16) * 16
    lanes = -(-max(win, rows + taps - 1) // 128) * 128
    as_rows = filters_low.astype(jnp.float32)
    ahead = jnp.pad(as_rows[:, ::-1], ((0, 0), (0, lanes - taps))).reshape(groups, 1, lanes)
    behind = jnp.pad(as_rows, ((0, 0), (0, lanes - taps))).reshape(groups, 1, lanes)
    pw = jnp.pad(product, ((0, 0), (0, lanes - win))).reshape(groups, channels // groups, lanes)
    gw = jnp.pad(grad_mixed, ((0, 0), (0, lanes - win))).reshape(groups, channels // groups, lanes)
    step = math.gcd(groups, 4)
    size = channels // groups

    def blocks(*tail):
        return pl.BlockSpec((step,) + tail, lambda i: (i, 0, 0))

    fo, bo, fg = pl.pallas_call(
        functools.partial(banded_kernel, here=here),
        out_shape=(jax.ShapeDtypeStruct((groups, size, rows), jnp.float32),) * 2
        + (jax.ShapeDtypeStruct((groups, 1, taps), jnp.float32),),
        grid=(groups // step,),
        in_specs=[blocks(1, lanes), blocks(1, lanes), blocks(size, lanes), blocks(size, lanes)],
        out_specs=(blocks(size, rows), blocks(size, rows), blocks(1, taps)),
        compiler_params=pltpu.CompilerParams(vmem_limit_bytes=8 * 1024 * 1024),
        cost_estimate=pl.CostEstimate(
            flops=4 * channels * lanes * (rows + here), transcendentals=0, bytes_accessed=4 * channels * (lanes + 2 * rows)
        ),
    )(ahead, behind, pw, gw)
    return fo.reshape(channels, rows)[:, :out_len], bo.reshape(channels, rows)[:, :out_len], fg.reshape(groups, taps)


def shards(outer_gate, inner_gate, value_stream, grad_output, filters, feature_taps, skip_gain):
    channels, block_len = outer_gate.shape
    ctx_size = lax.axis_size("ctx")
    fsdp_size = lax.axis_size("fsdp")
    n_dev = ctx_size * fsdp_size
    groups, taps_here = filters.shape
    taps_count = taps_here * ctx_size
    reach_cols = taps_count - 1
    group_size = channels // groups
    chunk = feature_taps.shape[2]

    row = jnp.concatenate([filters.reshape(-1), feature_taps.reshape(-1), skip_gain])
    gathered = lax.all_to_all(
        jnp.broadcast_to(row[None], (ctx_size, row.shape[0])), "ctx", 0, 0, tiled=True
    )
    n_filt = groups * taps_here
    n_chunk = row.shape[0] - n_filt
    per_block = ctx_size // fsdp_size
    filters_all = (
        gathered[:, :n_filt]
        .reshape(ctx_size, groups, taps_here)
        .transpose(1, 0, 2)
        .reshape(groups, taps_count)
    )
    moved = lax.all_to_all(gathered[:, n_filt:], "fsdp", 0, 0, tiled=True)
    local = (
        moved.reshape(fsdp_size, per_block, n_chunk).transpose(1, 0, 2).reshape(ctx_size, n_chunk)
    )
    taps_all = (
        local[:, : 9 * chunk].reshape(ctx_size, 3, 3, chunk).transpose(1, 2, 0, 3).reshape(3, 3, channels)
    )
    skip_all = local[:, 9 * chunk :].reshape(channels)

    rim = reach_cols + 2
    prev_rim = passed_along(
        jnp.concatenate(
            [outer_gate[:, block_len - 2 :], inner_gate[:, block_len - rim :], value_stream[:, block_len - rim :]],
            axis=1,
        ),
        "ctx",
        1,
    )
    next_rim = passed_along(
        jnp.concatenate(
            [grad_output[:, :rim], outer_gate[:, :rim], inner_gate[:, :2], value_stream[:, :2]], axis=1
        ),
        "ctx",
        -1,
    )
    outer_ext = jnp.concatenate([prev_rim[:, :2], outer_gate, next_rim[:, rim : 2 * rim]], axis=1)
    inner_ext = jnp.concatenate(
        [prev_rim[:, 2 : 2 + rim], inner_gate, next_rim[:, 2 * rim : 2 * rim + 2]], axis=1
    )
    value_ext = jnp.concatenate([prev_rim[:, 2 + rim :], value_stream, next_rim[:, 2 * rim + 2 :]], axis=1)
    upstream = jnp.concatenate([grad_output, next_rim[:, :rim]], axis=1).astype(jnp.float32)

    outer_feat = featurize(outer_ext.astype(jnp.float32), taps_all[0])
    inner_feat = featurize(inner_ext.astype(jnp.float32), taps_all[1])
    value_feat = featurize(value_ext.astype(jnp.float32), taps_all[2])
    product = (inner_feat * value_feat).astype(jnp.bfloat16)

    out_len = block_len + 2
    filters_low = filters_all.astype(jnp.bfloat16)
    product_here = product[:, reach_cols:].astype(jnp.float32)
    grad_mixed = (upstream * outer_feat).astype(jnp.bfloat16)
    convolved, ahead, filter_diag = both_convs(product, grad_mixed, filters_low, block_len)
    mixed = convolved + skip_all[:, None] * product_here

    grad_outer_feat = (upstream[:, :out_len] * mixed).astype(jnp.bfloat16)
    grad_product = ahead + skip_all[:, None] * grad_mixed[:, :out_len].astype(jnp.float32)
    grad_inner_feat = (grad_product * value_feat[:, reach_cols:]).astype(jnp.bfloat16)
    grad_value_feat = (grad_product * inner_feat[:, reach_cols:]).astype(jnp.bfloat16)

    grad_scale = 1.0 / math.sqrt(ctx_size * block_len)
    gm_here = grad_mixed[:, :block_len]
    filter_part = grad_scale * filter_diag[:, ::-1]
    skip_part = grad_scale * jnp.sum(
        gm_here.astype(jnp.float32) * product_here[:, :block_len], axis=1
    )
    taps_part = grad_scale * jnp.stack(
        [
            tap_sums(grad_outer_feat[:, :block_len], outer_ext[:, : block_len + 2]),
            tap_sums(grad_inner_feat[:, :block_len], inner_ext[:, reach_cols : reach_cols + block_len + 2]),
            tap_sums(grad_value_feat[:, :block_len], value_ext[:, reach_cols : reach_cols + block_len + 2]),
        ]
    )

    chunk_parts = jnp.concatenate(
        [
            taps_part.reshape(3, 3, ctx_size, chunk).transpose(2, 0, 1, 3).reshape(ctx_size, -1),
            skip_part.reshape(ctx_size, chunk),
        ],
        axis=1,
    )
    to_fsdp = chunk_parts.reshape(per_block, fsdp_size, n_chunk).transpose(1, 0, 2).reshape(ctx_size, n_chunk)
    to_fsdp, outer_feat, mixed, grad_outer_feat = lax.optimization_barrier(
        (to_fsdp, outer_feat, mixed, grad_outer_feat)
    )
    by_owner = lax.all_to_all(to_fsdp, "fsdp", 0, 0, tiled=True)
    gated_out = (outer_feat[:, :block_len] * mixed[:, :block_len]).astype(jnp.bfloat16)
    grad_outer = carry_back(grad_outer_feat.astype(jnp.float32), taps_all[0])
    by_owner, grad_inner_feat, grad_value_feat = lax.optimization_barrier(
        (by_owner, grad_inner_feat, grad_value_feat)
    )
    grad_inner = carry_back(grad_inner_feat.astype(jnp.float32), taps_all[1])
    grad_value = carry_back(grad_value_feat.astype(jnp.float32), taps_all[2])

    send = jnp.concatenate(
        [
            filter_part.reshape(groups, ctx_size, taps_here).transpose(1, 0, 2).reshape(ctx_size, -1),
            by_owner,
        ],
        axis=1,
    )
    reduced = jnp.sum(lax.all_to_all(send, "ctx", 0, 0, tiled=True), axis=0)
    filter_share = reduced[:n_filt].reshape(groups, taps_here)
    taps_share = reduced[n_filt : n_filt + 9 * chunk].reshape(3, 3, chunk)
    skip_share = reduced[n_filt + 9 * chunk :]
    return (
        gated_out,
        grad_outer.astype(jnp.bfloat16),
        grad_inner.astype(jnp.bfloat16),
        grad_value.astype(jnp.bfloat16),
        filter_share,
        taps_share,
        skip_share,
    )


def solution(mesh):
    return jax.shard_map(
        shards,
        mesh=mesh,
        in_specs=(
            P("fsdp", "ctx"),
            P("fsdp", "ctx"),
            P("fsdp", "ctx"),
            P("fsdp", "ctx"),
            P("fsdp", "ctx"),
            P(None, None, ("ctx", "fsdp")),
            P(("ctx", "fsdp")),
        ),
        out_specs=(
            P("fsdp", "ctx"),
            P("fsdp", "ctx"),
            P("fsdp", "ctx"),
            P("fsdp", "ctx"),
            P("fsdp", "ctx"),
            P(None, None, ("ctx", "fsdp")),
            P(("ctx", "fsdp")),
        ),
        check_vma=False,
    )
```

```python
import functools
import math

import jax
import jax.numpy as jnp
from jax import lax
from jax.experimental import pallas as pl
from jax.experimental.pallas import tpu as pltpu
from jax.sharding import PartitionSpec as P


def passed_along(shard, axis, by):
    devices = lax.axis_size(axis)
    pairs = [(i, i + by) for i in range(devices) if 0 <= i + by < devices]
    return lax.ppermute(shard, axis, pairs)


def featurize(extended, tap_gains):
    out_len = extended.shape[1] - 2
    result = tap_gains[0][:, None] * extended[:, 2:]
    result = result + tap_gains[1][:, None] * extended[:, 1 : out_len + 1]
    return result + tap_gains[2][:, None] * extended[:, :out_len]


def carry_back(extended, tap_gains):
    out_len = extended.shape[1] - 2
    result = tap_gains[0][:, None] * extended[:, :out_len]
    result = result + tap_gains[1][:, None] * extended[:, 1 : out_len + 1]
    return result + tap_gains[2][:, None] * extended[:, 2:]


def tap_sums(grad_rows, extended):
    block_len = grad_rows.shape[1]
    weighted = grad_rows.astype(jnp.float32)
    return jnp.stack(
        [
            jnp.sum(
                weighted * extended[:, 2 - shift_by : 2 - shift_by + block_len].astype(jnp.float32),
                axis=1,
            )
            for shift_by in range(3)
        ]
    )


def toeplitz_rows(filters_low, out_len):
    groups, taps_count = filters_low.shape
    window = out_len + taps_count - 1
    filter_row = jnp.concatenate(
        [filters_low[:, ::-1], jnp.zeros((groups, window + 1 - taps_count), filters_low.dtype)],
        axis=1,
    )
    flattened = jnp.tile(filter_row, (1, out_len))[:, : out_len * window]
    return flattened.reshape(groups, out_len, window)


def skew_sum(cross_terms, taps_count):
    groups, block_len, window = cross_terms.shape
    flattened = jnp.pad(cross_terms.reshape(groups, block_len * window), ((0, 0), (0, block_len)))
    return jnp.sum(flattened.reshape(groups, block_len, window + 1)[:, :, :taps_count], axis=1)[
        :, ::-1
    ]


def depthwise(values, kernel):
    channels = values.shape[0]
    return lax.conv_general_dilated(
        values[None],
        kernel[:, None, :],
        window_strides=(1,),
        padding="VALID",
        dimension_numbers=("NCH", "OIH", "NCH"),
        feature_group_count=channels,
        preferred_element_type=jnp.float32,
    )[0]


def banded_kernel(ahead_ref, behind_ref, pw_ref, gw_ref, fo_ref, bo_ref, fg_ref, *, here):
    rows = fo_ref.shape[2]
    lanes = ahead_ref.shape[2]
    dims = (((1,), (1,)), ((), ()))
    flip = (
        lax.broadcasted_iota(jnp.int32, (here, here), 0) + lax.broadcasted_iota(jnp.int32, (here, here), 1)
        == here - 1
    ).astype(jnp.bfloat16)
    for group in range(ahead_ref.shape[0]):
        for row_ref, data_ref, out_ref in ((ahead_ref, pw_ref, fo_ref), (behind_ref, gw_ref, bo_ref)):
            band = pltpu.roll(
                jnp.broadcast_to(row_ref[group], (rows, lanes)), 0, 1, stride=1, stride_axis=0
            ).astype(jnp.bfloat16)
            out_ref[group] = lax.dot_general(
                data_ref[group], band, dims, preferred_element_type=jnp.float32
            )
        gm_rev = jnp.dot(gw_ref[group][:, :here], flip, preferred_element_type=jnp.float32).astype(jnp.bfloat16)
        cross = lax.dot_general(
            gm_rev, pw_ref[group], (((0,), (0,)), ((), ())), preferred_element_type=jnp.float32
        )
        diag = pltpu.roll(cross, lanes - here + 1, 1, stride=1, stride_axis=0)
        fg_ref[group] = jnp.sum(diag, axis=0, keepdims=True)[:, : fg_ref.shape[2]]


def both_convs(product, grad_mixed, filters_low, here):
    channels, win = product.shape
    groups, taps = filters_low.shape
    out_len = win - taps + 1
    rows = -(-out_len // 16) * 16
    lanes = -(-max(win, rows + taps - 1) // 128) * 128
    as_rows = filters_low.astype(jnp.float32)
    ahead = jnp.pad(as_rows[:, ::-1], ((0, 0), (0, lanes - taps))).reshape(groups, 1, lanes)
    behind = jnp.pad(as_rows, ((0, 0), (0, lanes - taps))).reshape(groups, 1, lanes)
    pw = jnp.pad(product, ((0, 0), (0, lanes - win))).reshape(groups, channels // groups, lanes)
    gw = jnp.pad(grad_mixed, ((0, 0), (0, lanes - win))).reshape(groups, channels // groups, lanes)
    step = math.gcd(groups, 4)
    size = channels // groups

    def blocks(*tail):
        return pl.BlockSpec((step,) + tail, lambda i: (i, 0, 0))

    fo, bo, fg = pl.pallas_call(
        functools.partial(banded_kernel, here=here),
        out_shape=(jax.ShapeDtypeStruct((groups, size, rows), jnp.float32),) * 2
        + (jax.ShapeDtypeStruct((groups, 1, taps), jnp.float32),),
        grid=(groups // step,),
        in_specs=[blocks(1, lanes), blocks(1, lanes), blocks(size, lanes), blocks(size, lanes)],
        out_specs=(blocks(size, rows), blocks(size, rows), blocks(1, taps)),
        compiler_params=pltpu.CompilerParams(vmem_limit_bytes=8 * 1024 * 1024),
        cost_estimate=pl.CostEstimate(
            flops=4 * channels * lanes * (rows + here), transcendentals=0, bytes_accessed=4 * channels * (lanes + 2 * rows)
        ),
    )(ahead, behind, pw, gw)
    return fo.reshape(channels, rows)[:, :out_len], bo.reshape(channels, rows)[:, :out_len], fg.reshape(groups, taps)


def shards(outer_gate, inner_gate, value_stream, grad_output, filters, feature_taps, skip_gain):
    channels, block_len = outer_gate.shape
    ctx_size = lax.axis_size("ctx")
    fsdp_size = lax.axis_size("fsdp")
    n_dev = ctx_size * fsdp_size
    groups, taps_here = filters.shape
    taps_count = taps_here * ctx_size
    reach_cols = taps_count - 1
    group_size = channels // groups
    chunk = feature_taps.shape[2]

    row = jnp.concatenate([filters.reshape(-1), feature_taps.reshape(-1), skip_gain])
    gathered = lax.all_to_all(
        jnp.broadcast_to(row[None], (ctx_size, row.shape[0])), "ctx", 0, 0, tiled=True
    )
    n_filt = groups * taps_here
    n_chunk = row.shape[0] - n_filt
    per_block = ctx_size // fsdp_size
    filters_all = (
        gathered[:, :n_filt]
        .reshape(ctx_size, groups, taps_here)
        .transpose(1, 0, 2)
        .reshape(groups, taps_count)
    )
    chunk_rows, outer_gate, inner_gate, value_stream, grad_output = lax.optimization_barrier(
        (gathered[:, n_filt:], outer_gate, inner_gate, value_stream, grad_output)
    )
    moved = lax.all_to_all(chunk_rows, "fsdp", 0, 0, tiled=True)
    rim = reach_cols + 2
    prev_rim = passed_along(
        jnp.concatenate(
            [outer_gate[:, block_len - 2 :], inner_gate[:, block_len - rim :], value_stream[:, block_len - rim :]],
            axis=1,
        ),
        "ctx",
        1,
    )
    next_rim = passed_along(
        jnp.concatenate(
            [grad_output[:, :rim], outer_gate[:, :rim], inner_gate[:, :2], value_stream[:, :2]], axis=1
        ),
        "ctx",
        -1,
    )
    local = (
        moved.reshape(fsdp_size, per_block, n_chunk).transpose(1, 0, 2).reshape(ctx_size, n_chunk)
    )
    taps_all = (
        local[:, : 9 * chunk].reshape(ctx_size, 3, 3, chunk).transpose(1, 2, 0, 3).reshape(3, 3, channels)
    )
    skip_all = local[:, 9 * chunk :].reshape(channels)

    outer_ext = jnp.concatenate([prev_rim[:, :2], outer_gate, next_rim[:, rim : 2 * rim]], axis=1)
    inner_ext = jnp.concatenate(
        [prev_rim[:, 2 : 2 + rim], inner_gate, next_rim[:, 2 * rim : 2 * rim + 2]], axis=1
    )
    value_ext = jnp.concatenate([prev_rim[:, 2 + rim :], value_stream, next_rim[:, 2 * rim + 2 :]], axis=1)
    upstream = jnp.concatenate([grad_output, next_rim[:, :rim]], axis=1).astype(jnp.float32)

    outer_feat = featurize(outer_ext.astype(jnp.float32), taps_all[0])
    inner_feat = featurize(inner_ext.astype(jnp.float32), taps_all[1])
    value_feat = featurize(value_ext.astype(jnp.float32), taps_all[2])
    product = (inner_feat * value_feat).astype(jnp.bfloat16)

    out_len = block_len + 2
    filters_low = filters_all.astype(jnp.bfloat16)
    product_here = product[:, reach_cols:].astype(jnp.float32)
    grad_mixed = (upstream * outer_feat).astype(jnp.bfloat16)
    convolved, ahead, filter_diag = both_convs(product, grad_mixed, filters_low, block_len)
    mixed = convolved + skip_all[:, None] * product_here

    grad_outer_feat = (upstream[:, :out_len] * mixed).astype(jnp.bfloat16)
    grad_product = ahead + skip_all[:, None] * grad_mixed[:, :out_len].astype(jnp.float32)
    grad_inner_feat = (grad_product * value_feat[:, reach_cols:]).astype(jnp.bfloat16)
    grad_value_feat = (grad_product * inner_feat[:, reach_cols:]).astype(jnp.bfloat16)

    grad_scale = 1.0 / math.sqrt(ctx_size * block_len)
    gm_here = grad_mixed[:, :block_len]
    filter_part = grad_scale * filter_diag[:, ::-1]
    skip_part = grad_scale * jnp.sum(
        gm_here.astype(jnp.float32) * product_here[:, :block_len], axis=1
    )
    taps_part = grad_scale * jnp.stack(
        [
            tap_sums(grad_outer_feat[:, :block_len], outer_ext[:, : block_len + 2]),
            tap_sums(grad_inner_feat[:, :block_len], inner_ext[:, reach_cols : reach_cols + block_len + 2]),
            tap_sums(grad_value_feat[:, :block_len], value_ext[:, reach_cols : reach_cols + block_len + 2]),
        ]
    )

    chunk_parts = jnp.concatenate(
        [
            taps_part.reshape(3, 3, ctx_size, chunk).transpose(2, 0, 1, 3).reshape(ctx_size, -1),
            skip_part.reshape(ctx_size, chunk),
        ],
        axis=1,
    )
    to_fsdp = chunk_parts.reshape(per_block, fsdp_size, n_chunk).transpose(1, 0, 2).reshape(ctx_size, n_chunk)
    to_fsdp, outer_feat, mixed, grad_outer_feat = lax.optimization_barrier(
        (to_fsdp, outer_feat, mixed, grad_outer_feat)
    )
    by_owner = lax.all_to_all(to_fsdp, "fsdp", 0, 0, tiled=True)
    gated_out = (outer_feat[:, :block_len] * mixed[:, :block_len]).astype(jnp.bfloat16)
    grad_outer = carry_back(grad_outer_feat.astype(jnp.float32), taps_all[0])
    by_owner, grad_inner_feat, grad_value_feat = lax.optimization_barrier(
        (by_owner, grad_inner_feat, grad_value_feat)
    )
    grad_inner = carry_back(grad_inner_feat.astype(jnp.float32), taps_all[1])
    grad_value = carry_back(grad_value_feat.astype(jnp.float32), taps_all[2])

    send = jnp.concatenate(
        [
            filter_part.reshape(groups, ctx_size, taps_here).transpose(1, 0, 2).reshape(ctx_size, -1),
            by_owner,
        ],
        axis=1,
    )
    reduced = jnp.sum(lax.all_to_all(send, "ctx", 0, 0, tiled=True), axis=0)
    filter_share = reduced[:n_filt].reshape(groups, taps_here)
    taps_share = reduced[n_filt : n_filt + 9 * chunk].reshape(3, 3, chunk)
    skip_share = reduced[n_filt + 9 * chunk :]
    return (
        gated_out,
        grad_outer.astype(jnp.bfloat16),
        grad_inner.astype(jnp.bfloat16),
        grad_value.astype(jnp.bfloat16),
        filter_share,
        taps_share,
        skip_share,
    )


def solution(mesh):
    return jax.shard_map(
        shards,
        mesh=mesh,
        in_specs=(
            P("fsdp", "ctx"),
            P("fsdp", "ctx"),
            P("fsdp", "ctx"),
            P("fsdp", "ctx"),
            P("fsdp", "ctx"),
            P(None, None, ("ctx", "fsdp")),
            P(("ctx", "fsdp")),
        ),
        out_specs=(
            P("fsdp", "ctx"),
            P("fsdp", "ctx"),
            P("fsdp", "ctx"),
            P("fsdp", "ctx"),
            P("fsdp", "ctx"),
            P(None, None, ("ctx", "fsdp")),
            P(("ctx", "fsdp")),
        ),
        check_vma=False,
    )
```

```python
import functools
import math

import jax
import jax.numpy as jnp
from jax import lax
from jax.experimental import pallas as pl
from jax.experimental.pallas import tpu as pltpu
from jax.sharding import PartitionSpec as P


def passed_along(shard, axis, by):
    devices = lax.axis_size(axis)
    pairs = [(i, i + by) for i in range(devices) if 0 <= i + by < devices]
    return lax.ppermute(shard, axis, pairs)


def featurize(extended, tap_gains):
    out_len = extended.shape[1] - 2
    result = tap_gains[0][:, None] * extended[:, 2:]
    result = result + tap_gains[1][:, None] * extended[:, 1 : out_len + 1]
    return result + tap_gains[2][:, None] * extended[:, :out_len]


def carry_back(extended, tap_gains):
    out_len = extended.shape[1] - 2
    result = tap_gains[0][:, None] * extended[:, :out_len]
    result = result + tap_gains[1][:, None] * extended[:, 1 : out_len + 1]
    return result + tap_gains[2][:, None] * extended[:, 2:]


def tap_sums(grad_rows, extended):
    block_len = grad_rows.shape[1]
    weighted = grad_rows.astype(jnp.float32)
    return jnp.stack(
        [
            jnp.sum(
                weighted * extended[:, 2 - shift_by : 2 - shift_by + block_len].astype(jnp.float32),
                axis=1,
            )
            for shift_by in range(3)
        ]
    )


def toeplitz_rows(filters_low, out_len):
    groups, taps_count = filters_low.shape
    window = out_len + taps_count - 1
    filter_row = jnp.concatenate(
        [filters_low[:, ::-1], jnp.zeros((groups, window + 1 - taps_count), filters_low.dtype)],
        axis=1,
    )
    flattened = jnp.tile(filter_row, (1, out_len))[:, : out_len * window]
    return flattened.reshape(groups, out_len, window)


def skew_sum(cross_terms, taps_count):
    groups, block_len, window = cross_terms.shape
    flattened = jnp.pad(cross_terms.reshape(groups, block_len * window), ((0, 0), (0, block_len)))
    return jnp.sum(flattened.reshape(groups, block_len, window + 1)[:, :, :taps_count], axis=1)[
        :, ::-1
    ]


def depthwise(values, kernel):
    channels = values.shape[0]
    return lax.conv_general_dilated(
        values[None],
        kernel[:, None, :],
        window_strides=(1,),
        padding="VALID",
        dimension_numbers=("NCH", "OIH", "NCH"),
        feature_group_count=channels,
        preferred_element_type=jnp.float32,
    )[0]


def banded_kernel(ahead_ref, behind_ref, pw_ref, gw_ref, fo_ref, bo_ref, fg_ref, *, here):
    rows = fo_ref.shape[2]
    lanes = ahead_ref.shape[2]
    dims = (((1,), (1,)), ((), ()))
    flip = (
        lax.broadcasted_iota(jnp.int32, (here, here), 0) + lax.broadcasted_iota(jnp.int32, (here, here), 1)
        == here - 1
    ).astype(jnp.bfloat16)
    for group in range(ahead_ref.shape[0]):
        for row_ref, data_ref, out_ref in ((ahead_ref, pw_ref, fo_ref), (behind_ref, gw_ref, bo_ref)):
            band = pltpu.roll(
                jnp.broadcast_to(row_ref[group], (rows, lanes)), 0, 1, stride=1, stride_axis=0
            ).astype(jnp.bfloat16)
            out_ref[group] = lax.dot_general(
                data_ref[group], band, dims, preferred_element_type=jnp.float32
            )
        gm_rev = jnp.dot(gw_ref[group][:, :here], flip, preferred_element_type=jnp.float32).astype(jnp.bfloat16)
        cross = lax.dot_general(
            gm_rev, pw_ref[group], (((0,), (0,)), ((), ())), preferred_element_type=jnp.float32
        )
        diag = pltpu.roll(cross, lanes - here + 1, 1, stride=1, stride_axis=0)
        fg_ref[group] = jnp.sum(diag, axis=0, keepdims=True)[:, : fg_ref.shape[2]]


def both_convs(product, grad_mixed, filters_low, here):
    channels, win = product.shape
    groups, taps = filters_low.shape
    out_len = win - taps + 1
    rows = -(-out_len // 16) * 16
    lanes = -(-max(win, rows + taps - 1) // 128) * 128
    as_rows = filters_low.astype(jnp.float32)
    ahead = jnp.pad(as_rows[:, ::-1], ((0, 0), (0, lanes - taps))).reshape(groups, 1, lanes)
    behind = jnp.pad(as_rows, ((0, 0), (0, lanes - taps))).reshape(groups, 1, lanes)
    pw = jnp.pad(product, ((0, 0), (0, lanes - win))).reshape(groups, channels // groups, lanes)
    gw = jnp.pad(grad_mixed, ((0, 0), (0, lanes - win))).reshape(groups, channels // groups, lanes)
    step = math.gcd(groups, 4)
    size = channels // groups

    def blocks(*tail):
        return pl.BlockSpec((step,) + tail, lambda i: (i, 0, 0))

    fo, bo, fg = pl.pallas_call(
        functools.partial(banded_kernel, here=here),
        out_shape=(jax.ShapeDtypeStruct((groups, size, rows), jnp.float32),) * 2
        + (jax.ShapeDtypeStruct((groups, 1, taps), jnp.float32),),
        grid=(groups // step,),
        in_specs=[blocks(1, lanes), blocks(1, lanes), blocks(size, lanes), blocks(size, lanes)],
        out_specs=(blocks(size, rows), blocks(size, rows), blocks(1, taps)),
        compiler_params=pltpu.CompilerParams(vmem_limit_bytes=8 * 1024 * 1024),
        cost_estimate=pl.CostEstimate(
            flops=4 * channels * lanes * (rows + here), transcendentals=0, bytes_accessed=4 * channels * (lanes + 2 * rows)
        ),
    )(ahead, behind, pw, gw)
    return fo.reshape(channels, rows)[:, :out_len], bo.reshape(channels, rows)[:, :out_len], fg.reshape(groups, taps)


def shards(outer_gate, inner_gate, value_stream, grad_output, filters, feature_taps, skip_gain):
    channels, block_len = outer_gate.shape
    ctx_size = lax.axis_size("ctx")
    fsdp_size = lax.axis_size("fsdp")
    n_dev = ctx_size * fsdp_size
    groups, taps_here = filters.shape
    taps_count = taps_here * ctx_size
    reach_cols = taps_count - 1
    group_size = channels // groups
    chunk = feature_taps.shape[2]

    row = jnp.concatenate([filters.reshape(-1), feature_taps.reshape(-1), skip_gain])
    gathered = lax.all_to_all(
        jnp.broadcast_to(row[None], (ctx_size, row.shape[0])), "ctx", 0, 0, tiled=True
    )
    n_filt = groups * taps_here
    n_chunk = row.shape[0] - n_filt
    per_block = ctx_size // fsdp_size
    filters_all = (
        gathered[:, :n_filt]
        .reshape(ctx_size, groups, taps_here)
        .transpose(1, 0, 2)
        .reshape(groups, taps_count)
    )
    moved = lax.all_to_all(gathered[:, n_filt:], "fsdp", 0, 0, tiled=True)
    local = (
        moved.reshape(fsdp_size, per_block, n_chunk).transpose(1, 0, 2).reshape(ctx_size, n_chunk)
    )
    taps_all = (
        local[:, : 9 * chunk].reshape(ctx_size, 3, 3, chunk).transpose(1, 2, 0, 3).reshape(3, 3, channels)
    )
    skip_all = local[:, 9 * chunk :].reshape(channels)

    rim = reach_cols + 2
    prev_rim = passed_along(
        jnp.concatenate(
            [outer_gate[:, block_len - 2 :], inner_gate[:, block_len - rim :], value_stream[:, block_len - rim :]],
            axis=1,
        ),
        "ctx",
        1,
    )
    next_rim = passed_along(
        jnp.concatenate(
            [grad_output[:, :rim], outer_gate[:, :rim], inner_gate[:, :2], value_stream[:, :2]], axis=1
        ),
        "ctx",
        -1,
    )
    outer_ext = jnp.concatenate([prev_rim[:, :2], outer_gate, next_rim[:, rim : 2 * rim]], axis=1)
    inner_ext = jnp.concatenate(
        [prev_rim[:, 2 : 2 + rim], inner_gate, next_rim[:, 2 * rim : 2 * rim + 2]], axis=1
    )
    value_ext = jnp.concatenate([prev_rim[:, 2 + rim :], value_stream, next_rim[:, 2 * rim + 2 :]], axis=1)
    upstream = jnp.concatenate([grad_output, next_rim[:, :rim]], axis=1).astype(jnp.float32)

    outer_feat = featurize(outer_ext.astype(jnp.float32), taps_all[0])
    inner_feat = featurize(inner_ext.astype(jnp.float32), taps_all[1])
    value_feat = featurize(value_ext.astype(jnp.float32), taps_all[2])
    product = (inner_feat * value_feat).astype(jnp.bfloat16)

    out_len = block_len + 2
    filters_low = filters_all.astype(jnp.bfloat16)
    product_here = product[:, reach_cols:].astype(jnp.float32)
    grad_mixed = (upstream * outer_feat).astype(jnp.bfloat16)
    convolved, ahead, filter_diag = both_convs(product, grad_mixed, filters_low, block_len)
    mixed = convolved + skip_all[:, None] * product_here

    grad_outer_feat = (upstream[:, :out_len] * mixed).astype(jnp.bfloat16)
    grad_product = ahead + skip_all[:, None] * grad_mixed[:, :out_len].astype(jnp.float32)
    grad_inner_feat = (grad_product * value_feat[:, reach_cols:]).astype(jnp.bfloat16)
    grad_value_feat = (grad_product * inner_feat[:, reach_cols:]).astype(jnp.bfloat16)

    grad_scale = 1.0 / math.sqrt(ctx_size * block_len)
    gm_here = grad_mixed[:, :block_len]
    filter_part = grad_scale * filter_diag[:, ::-1]
    skip_part = grad_scale * jnp.sum(
        gm_here.astype(jnp.float32) * product_here[:, :block_len], axis=1
    )
    taps_part = grad_scale * jnp.stack(
        [
            tap_sums(grad_outer_feat[:, :block_len], outer_ext[:, : block_len + 2]),
            tap_sums(grad_inner_feat[:, :block_len], inner_ext[:, reach_cols : reach_cols + block_len + 2]),
            tap_sums(grad_value_feat[:, :block_len], value_ext[:, reach_cols : reach_cols + block_len + 2]),
        ]
    )

    chunk_parts = jnp.concatenate(
        [
            taps_part.reshape(3, 3, ctx_size, chunk).transpose(2, 0, 1, 3).reshape(ctx_size, -1),
            skip_part.reshape(ctx_size, chunk),
        ],
        axis=1,
    )
    to_fsdp = chunk_parts.reshape(per_block, fsdp_size, n_chunk).transpose(1, 0, 2).reshape(ctx_size, n_chunk)
    to_fsdp, outer_feat, mixed, grad_outer_feat = lax.optimization_barrier(
        (to_fsdp, outer_feat, mixed, grad_outer_feat)
    )
    by_owner = lax.all_to_all(to_fsdp, "fsdp", 0, 0, tiled=True)
    gated_out = (outer_feat[:, :block_len] * mixed[:, :block_len]).astype(jnp.bfloat16)
    grad_outer = carry_back(grad_outer_feat.astype(jnp.float32), taps_all[0])
    by_owner, grad_inner_feat, grad_value_feat = lax.optimization_barrier(
        (by_owner, grad_inner_feat, grad_value_feat)
    )
    grad_inner = carry_back(grad_inner_feat.astype(jnp.float32), taps_all[1])
    grad_value = carry_back(grad_value_feat.astype(jnp.float32), taps_all[2])

    send = jnp.concatenate(
        [
            filter_part.reshape(groups, ctx_size, taps_here).transpose(1, 0, 2).reshape(ctx_size, -1),
            by_owner,
        ],
        axis=1,
    )
    arrived = lax.all_to_all(send, "ctx", 0, 0, tiled=True)
    filter_share = jnp.sum(arrived[:, :n_filt], axis=0).reshape(groups, taps_here)
    taps_share = jnp.sum(arrived[:, n_filt : n_filt + 9 * chunk], axis=0).reshape(3, 3, chunk)
    skip_share = jnp.sum(arrived[:, n_filt + 9 * chunk :], axis=0)
    return (
        gated_out,
        grad_outer.astype(jnp.bfloat16),
        grad_inner.astype(jnp.bfloat16),
        grad_value.astype(jnp.bfloat16),
        filter_share,
        taps_share,
        skip_share,
    )


def solution(mesh):
    return jax.shard_map(
        shards,
        mesh=mesh,
        in_specs=(
            P("fsdp", "ctx"),
            P("fsdp", "ctx"),
            P("fsdp", "ctx"),
            P("fsdp", "ctx"),
            P("fsdp", "ctx"),
            P(None, None, ("ctx", "fsdp")),
            P(("ctx", "fsdp")),
        ),
        out_specs=(
            P("fsdp", "ctx"),
            P("fsdp", "ctx"),
            P("fsdp", "ctx"),
            P("fsdp", "ctx"),
            P("fsdp", "ctx"),
            P(None, None, ("ctx", "fsdp")),
            P(("ctx", "fsdp")),
        ),
        check_vma=False,
    )
```

```python
import functools
import math

import jax
import jax.numpy as jnp
from jax import lax
from jax.experimental import pallas as pl
from jax.experimental.pallas import tpu as pltpu
from jax.sharding import PartitionSpec as P


def passed_along(shard, axis, by):
    devices = lax.axis_size(axis)
    pairs = [(i, i + by) for i in range(devices) if 0 <= i + by < devices]
    return lax.ppermute(shard, axis, pairs)


def featurize(extended, tap_gains):
    out_len = extended.shape[1] - 2
    result = tap_gains[0][:, None] * extended[:, 2:]
    result = result + tap_gains[1][:, None] * extended[:, 1 : out_len + 1]
    return result + tap_gains[2][:, None] * extended[:, :out_len]


def carry_back(extended, tap_gains):
    out_len = extended.shape[1] - 2
    result = tap_gains[0][:, None] * extended[:, :out_len]
    result = result + tap_gains[1][:, None] * extended[:, 1 : out_len + 1]
    return result + tap_gains[2][:, None] * extended[:, 2:]


def tap_sums(grad_rows, extended):
    block_len = grad_rows.shape[1]
    weighted = grad_rows.astype(jnp.float32)
    return jnp.stack(
        [
            jnp.sum(
                weighted * extended[:, 2 - shift_by : 2 - shift_by + block_len].astype(jnp.float32),
                axis=1,
            )
            for shift_by in range(3)
        ]
    )


def toeplitz_rows(filters_low, out_len):
    groups, taps_count = filters_low.shape
    window = out_len + taps_count - 1
    filter_row = jnp.concatenate(
        [filters_low[:, ::-1], jnp.zeros((groups, window + 1 - taps_count), filters_low.dtype)],
        axis=1,
    )
    flattened = jnp.tile(filter_row, (1, out_len))[:, : out_len * window]
    return flattened.reshape(groups, out_len, window)


def skew_sum(cross_terms, taps_count):
    groups, block_len, window = cross_terms.shape
    flattened = jnp.pad(cross_terms.reshape(groups, block_len * window), ((0, 0), (0, block_len)))
    return jnp.sum(flattened.reshape(groups, block_len, window + 1)[:, :, :taps_count], axis=1)[
        :, ::-1
    ]


def depthwise(values, kernel):
    channels = values.shape[0]
    return lax.conv_general_dilated(
        values[None],
        kernel[:, None, :],
        window_strides=(1,),
        padding="VALID",
        dimension_numbers=("NCH", "OIH", "NCH"),
        feature_group_count=channels,
        preferred_element_type=jnp.float32,
    )[0]


def banded_kernel(ahead_ref, behind_ref, pw_ref, gw_ref, fo_ref, bo_ref, fg_ref, *, here):
    rows = fo_ref.shape[2]
    lanes = ahead_ref.shape[2]
    dims = (((1,), (1,)), ((), ()))
    flip = (
        lax.broadcasted_iota(jnp.int32, (here, here), 0) + lax.broadcasted_iota(jnp.int32, (here, here), 1)
        == here - 1
    ).astype(jnp.bfloat16)
    for group in range(ahead_ref.shape[0]):
        for row_ref, data_ref, out_ref in ((ahead_ref, pw_ref, fo_ref), (behind_ref, gw_ref, bo_ref)):
            band = pltpu.roll(
                jnp.broadcast_to(row_ref[group], (rows, lanes)), 0, 1, stride=1, stride_axis=0
            ).astype(jnp.bfloat16)
            out_ref[group] = lax.dot_general(
                data_ref[group], band, dims, preferred_element_type=jnp.float32
            )
        gm_rev = jnp.dot(gw_ref[group][:, :here], flip, preferred_element_type=jnp.float32).astype(jnp.bfloat16)
        cross = lax.dot_general(
            gm_rev, pw_ref[group], (((0,), (0,)), ((), ())), preferred_element_type=jnp.float32
        )
        diag = pltpu.roll(cross, lanes - here + 1, 1, stride=1, stride_axis=0)
        fg_ref[group] = jnp.sum(diag, axis=0, keepdims=True)[:, : fg_ref.shape[2]]


def both_convs(product, grad_mixed, filters_low, here):
    channels, win = product.shape
    groups, taps = filters_low.shape
    out_len = win - taps + 1
    rows = -(-out_len // 16) * 16
    lanes = -(-max(win, rows + taps - 1) // 128) * 128
    as_rows = filters_low.astype(jnp.float32)
    ahead = jnp.pad(as_rows[:, ::-1], ((0, 0), (0, lanes - taps))).reshape(groups, 1, lanes)
    behind = jnp.pad(as_rows, ((0, 0), (0, lanes - taps))).reshape(groups, 1, lanes)
    pw = jnp.pad(product, ((0, 0), (0, lanes - win))).reshape(groups, channels // groups, lanes)
    gw = jnp.pad(grad_mixed, ((0, 0), (0, lanes - win))).reshape(groups, channels // groups, lanes)
    step = math.gcd(groups, 8)
    size = channels // groups

    def blocks(*tail):
        return pl.BlockSpec((step,) + tail, lambda i: (i, 0, 0))

    fo, bo, fg = pl.pallas_call(
        functools.partial(banded_kernel, here=here),
        out_shape=(jax.ShapeDtypeStruct((groups, size, rows), jnp.float32),) * 2
        + (jax.ShapeDtypeStruct((groups, 1, taps), jnp.float32),),
        grid=(groups // step,),
        in_specs=[blocks(1, lanes), blocks(1, lanes), blocks(size, lanes), blocks(size, lanes)],
        out_specs=(blocks(size, rows), blocks(size, rows), blocks(1, taps)),
        compiler_params=pltpu.CompilerParams(vmem_limit_bytes=8 * 1024 * 1024),
        cost_estimate=pl.CostEstimate(
            flops=4 * channels * lanes * (rows + here), transcendentals=0, bytes_accessed=4 * channels * (lanes + 2 * rows)
        ),
    )(ahead, behind, pw, gw)
    return fo.reshape(channels, rows)[:, :out_len], bo.reshape(channels, rows)[:, :out_len], fg.reshape(groups, taps)


def shards(outer_gate, inner_gate, value_stream, grad_output, filters, feature_taps, skip_gain):
    channels, block_len = outer_gate.shape
    ctx_size = lax.axis_size("ctx")
    fsdp_size = lax.axis_size("fsdp")
    n_dev = ctx_size * fsdp_size
    groups, taps_here = filters.shape
    taps_count = taps_here * ctx_size
    reach_cols = taps_count - 1
    group_size = channels // groups
    chunk = feature_taps.shape[2]

    row = jnp.concatenate([filters.reshape(-1), feature_taps.reshape(-1), skip_gain])
    gathered = lax.all_to_all(
        jnp.broadcast_to(row[None], (ctx_size, row.shape[0])), "ctx", 0, 0, tiled=True
    )
    n_filt = groups * taps_here
    n_chunk = row.shape[0] - n_filt
    per_block = ctx_size // fsdp_size
    filters_all = (
        gathered[:, :n_filt]
        .reshape(ctx_size, groups, taps_here)
        .transpose(1, 0, 2)
        .reshape(groups, taps_count)
    )
    moved = lax.all_to_all(gathered[:, n_filt:], "fsdp", 0, 0, tiled=True)
    local = (
        moved.reshape(fsdp_size, per_block, n_chunk).transpose(1, 0, 2).reshape(ctx_size, n_chunk)
    )
    taps_all = (
        local[:, : 9 * chunk].reshape(ctx_size, 3, 3, chunk).transpose(1, 2, 0, 3).reshape(3, 3, channels)
    )
    skip_all = local[:, 9 * chunk :].reshape(channels)

    rim = reach_cols + 2
    prev_rim = passed_along(
        jnp.concatenate(
            [outer_gate[:, block_len - 2 :], inner_gate[:, block_len - rim :], value_stream[:, block_len - rim :]],
            axis=1,
        ),
        "ctx",
        1,
    )
    next_rim = passed_along(
        jnp.concatenate(
            [grad_output[:, :rim], outer_gate[:, :rim], inner_gate[:, :2], value_stream[:, :2]], axis=1
        ),
        "ctx",
        -1,
    )
    outer_ext = jnp.concatenate([prev_rim[:, :2], outer_gate, next_rim[:, rim : 2 * rim]], axis=1)
    inner_ext = jnp.concatenate(
        [prev_rim[:, 2 : 2 + rim], inner_gate, next_rim[:, 2 * rim : 2 * rim + 2]], axis=1
    )
    value_ext = jnp.concatenate([prev_rim[:, 2 + rim :], value_stream, next_rim[:, 2 * rim + 2 :]], axis=1)
    upstream = jnp.concatenate([grad_output, next_rim[:, :rim]], axis=1).astype(jnp.float32)

    outer_feat = featurize(outer_ext.astype(jnp.float32), taps_all[0])
    inner_feat = featurize(inner_ext.astype(jnp.float32), taps_all[1])
    value_feat = featurize(value_ext.astype(jnp.float32), taps_all[2])
    product = (inner_feat * value_feat).astype(jnp.bfloat16)

    out_len = block_len + 2
    filters_low = filters_all.astype(jnp.bfloat16)
    product_here = product[:, reach_cols:].astype(jnp.float32)
    grad_mixed = (upstream * outer_feat).astype(jnp.bfloat16)
    convolved, ahead, filter_diag = both_convs(product, grad_mixed, filters_low, block_len)
    mixed = convolved + skip_all[:, None] * product_here

    grad_outer_feat = (upstream[:, :out_len] * mixed).astype(jnp.bfloat16)
    grad_product = ahead + skip_all[:, None] * grad_mixed[:, :out_len].astype(jnp.float32)
    grad_inner_feat = (grad_product * value_feat[:, reach_cols:]).astype(jnp.bfloat16)
    grad_value_feat = (grad_product * inner_feat[:, reach_cols:]).astype(jnp.bfloat16)

    grad_scale = 1.0 / math.sqrt(ctx_size * block_len)
    gm_here = grad_mixed[:, :block_len]
    filter_part = grad_scale * filter_diag[:, ::-1]
    skip_part = grad_scale * jnp.sum(
        gm_here.astype(jnp.float32) * product_here[:, :block_len], axis=1
    )
    taps_part = grad_scale * jnp.stack(
        [
            tap_sums(grad_outer_feat[:, :block_len], outer_ext[:, : block_len + 2]),
            tap_sums(grad_inner_feat[:, :block_len], inner_ext[:, reach_cols : reach_cols + block_len + 2]),
            tap_sums(grad_value_feat[:, :block_len], value_ext[:, reach_cols : reach_cols + block_len + 2]),
        ]
    )

    chunk_parts = jnp.concatenate(
        [
            taps_part.reshape(3, 3, ctx_size, chunk).transpose(2, 0, 1, 3).reshape(ctx_size, -1),
            skip_part.reshape(ctx_size, chunk),
        ],
        axis=1,
    )
    to_fsdp = chunk_parts.reshape(per_block, fsdp_size, n_chunk).transpose(1, 0, 2).reshape(ctx_size, n_chunk)
    to_fsdp, outer_feat, mixed, grad_outer_feat = lax.optimization_barrier(
        (to_fsdp, outer_feat, mixed, grad_outer_feat)
    )
    by_owner = lax.all_to_all(to_fsdp, "fsdp", 0, 0, tiled=True)
    gated_out = (outer_feat[:, :block_len] * mixed[:, :block_len]).astype(jnp.bfloat16)
    grad_outer = carry_back(grad_outer_feat.astype(jnp.float32), taps_all[0])
    by_owner, grad_inner_feat, grad_value_feat = lax.optimization_barrier(
        (by_owner, grad_inner_feat, grad_value_feat)
    )
    grad_inner = carry_back(grad_inner_feat.astype(jnp.float32), taps_all[1])
    grad_value = carry_back(grad_value_feat.astype(jnp.float32), taps_all[2])

    send = jnp.concatenate(
        [
            filter_part.reshape(groups, ctx_size, taps_here).transpose(1, 0, 2).reshape(ctx_size, -1),
            by_owner,
        ],
        axis=1,
    )
    reduced = jnp.sum(lax.all_to_all(send, "ctx", 0, 0, tiled=True), axis=0)
    filter_share = reduced[:n_filt].reshape(groups, taps_here)
    taps_share = reduced[n_filt : n_filt + 9 * chunk].reshape(3, 3, chunk)
    skip_share = reduced[n_filt + 9 * chunk :]
    return (
        gated_out,
        grad_outer.astype(jnp.bfloat16),
        grad_inner.astype(jnp.bfloat16),
        grad_value.astype(jnp.bfloat16),
        filter_share,
        taps_share,
        skip_share,
    )


def solution(mesh):
    return jax.shard_map(
        shards,
        mesh=mesh,
        in_specs=(
            P("fsdp", "ctx"),
            P("fsdp", "ctx"),
            P("fsdp", "ctx"),
            P("fsdp", "ctx"),
            P("fsdp", "ctx"),
            P(None, None, ("ctx", "fsdp")),
            P(("ctx", "fsdp")),
        ),
        out_specs=(
            P("fsdp", "ctx"),
            P("fsdp", "ctx"),
            P("fsdp", "ctx"),
            P("fsdp", "ctx"),
            P("fsdp", "ctx"),
            P(None, None, ("ctx", "fsdp")),
            P(("ctx", "fsdp")),
        ),
        check_vma=False,
    )
```

```python
import functools
import math

import jax
import jax.numpy as jnp
from jax import lax
from jax.experimental import pallas as pl
from jax.experimental.pallas import tpu as pltpu
from jax.sharding import PartitionSpec as P


def passed_along(shard, axis, by):
    devices = lax.axis_size(axis)
    pairs = [(i, i + by) for i in range(devices) if 0 <= i + by < devices]
    return lax.ppermute(shard, axis, pairs)


def featurize(extended, tap_gains):
    out_len = extended.shape[1] - 2
    result = tap_gains[0][:, None] * extended[:, 2:]
    result = result + tap_gains[1][:, None] * extended[:, 1 : out_len + 1]
    return result + tap_gains[2][:, None] * extended[:, :out_len]


def carry_back(extended, tap_gains):
    out_len = extended.shape[1] - 2
    result = tap_gains[0][:, None] * extended[:, :out_len]
    result = result + tap_gains[1][:, None] * extended[:, 1 : out_len + 1]
    return result + tap_gains[2][:, None] * extended[:, 2:]


def tap_sums(grad_rows, extended):
    block_len = grad_rows.shape[1]
    weighted = grad_rows.astype(jnp.float32)
    return jnp.stack(
        [
            jnp.sum(
                weighted * extended[:, 2 - shift_by : 2 - shift_by + block_len].astype(jnp.float32),
                axis=1,
            )
            for shift_by in range(3)
        ]
    )


def toeplitz_rows(filters_low, out_len):
    groups, taps_count = filters_low.shape
    window = out_len + taps_count - 1
    filter_row = jnp.concatenate(
        [filters_low[:, ::-1], jnp.zeros((groups, window + 1 - taps_count), filters_low.dtype)],
        axis=1,
    )
    flattened = jnp.tile(filter_row, (1, out_len))[:, : out_len * window]
    return flattened.reshape(groups, out_len, window)


def skew_sum(cross_terms, taps_count):
    groups, block_len, window = cross_terms.shape
    flattened = jnp.pad(cross_terms.reshape(groups, block_len * window), ((0, 0), (0, block_len)))
    return jnp.sum(flattened.reshape(groups, block_len, window + 1)[:, :, :taps_count], axis=1)[
        :, ::-1
    ]


def depthwise(values, kernel):
    channels = values.shape[0]
    return lax.conv_general_dilated(
        values[None],
        kernel[:, None, :],
        window_strides=(1,),
        padding="VALID",
        dimension_numbers=("NCH", "OIH", "NCH"),
        feature_group_count=channels,
        preferred_element_type=jnp.float32,
    )[0]


def banded_kernel(ahead_ref, behind_ref, pw_ref, gw_ref, fo_ref, bo_ref, fg_ref, *, here):
    rows = fo_ref.shape[2]
    lanes = ahead_ref.shape[2]
    dims = (((1,), (1,)), ((), ()))
    flip = (
        lax.broadcasted_iota(jnp.int32, (here, here), 0) + lax.broadcasted_iota(jnp.int32, (here, here), 1)
        == here - 1
    ).astype(jnp.bfloat16)
    for group in range(ahead_ref.shape[0]):
        for row_ref, data_ref, out_ref in ((ahead_ref, pw_ref, fo_ref), (behind_ref, gw_ref, bo_ref)):
            band = pltpu.roll(
                jnp.broadcast_to(row_ref[group], (rows, lanes)), 0, 1, stride=1, stride_axis=0
            ).astype(jnp.bfloat16)
            out_ref[group] = lax.dot_general(
                data_ref[group], band, dims, preferred_element_type=jnp.float32
            )
        gm_rev = jnp.dot(gw_ref[group][:, :here], flip, preferred_element_type=jnp.float32).astype(jnp.bfloat16)
        cross = lax.dot_general(
            gm_rev, pw_ref[group], (((0,), (0,)), ((), ())), preferred_element_type=jnp.float32
        )
        diag = pltpu.roll(cross, lanes - here + 1, 1, stride=1, stride_axis=0)
        fg_ref[group] = jnp.sum(diag, axis=0, keepdims=True)[:, : fg_ref.shape[2]]


def both_convs(product, grad_mixed, filters_low, here):
    channels, win = product.shape
    groups, taps = filters_low.shape
    out_len = win - taps + 1
    rows = -(-out_len // 16) * 16
    lanes = -(-max(win, rows + taps - 1) // 128) * 128
    as_rows = filters_low.astype(jnp.float32)
    ahead = jnp.pad(as_rows[:, ::-1], ((0, 0), (0, lanes - taps))).reshape(groups, 1, lanes)
    behind = jnp.pad(as_rows, ((0, 0), (0, lanes - taps))).reshape(groups, 1, lanes)
    pw = jnp.pad(product, ((0, 0), (0, lanes - win))).reshape(groups, channels // groups, lanes)
    gw = jnp.pad(grad_mixed, ((0, 0), (0, lanes - win))).reshape(groups, channels // groups, lanes)
    step = groups
    size = channels // groups

    def blocks(*tail):
        return pl.BlockSpec((step,) + tail, lambda i: (i, 0, 0))

    fo, bo, fg = pl.pallas_call(
        functools.partial(banded_kernel, here=here),
        out_shape=(jax.ShapeDtypeStruct((groups, size, rows), jnp.float32),) * 2
        + (jax.ShapeDtypeStruct((groups, 1, taps), jnp.float32),),
        grid=(groups // step,),
        in_specs=[blocks(1, lanes), blocks(1, lanes), blocks(size, lanes), blocks(size, lanes)],
        out_specs=(blocks(size, rows), blocks(size, rows), blocks(1, taps)),
        compiler_params=pltpu.CompilerParams(vmem_limit_bytes=8 * 1024 * 1024),
        cost_estimate=pl.CostEstimate(
            flops=4 * channels * lanes * (rows + here), transcendentals=0, bytes_accessed=4 * channels * (lanes + 2 * rows)
        ),
    )(ahead, behind, pw, gw)
    return fo.reshape(channels, rows)[:, :out_len], bo.reshape(channels, rows)[:, :out_len], fg.reshape(groups, taps)


def shards(outer_gate, inner_gate, value_stream, grad_output, filters, feature_taps, skip_gain):
    channels, block_len = outer_gate.shape
    ctx_size = lax.axis_size("ctx")
    fsdp_size = lax.axis_size("fsdp")
    n_dev = ctx_size * fsdp_size
    groups, taps_here = filters.shape
    taps_count = taps_here * ctx_size
    reach_cols = taps_count - 1
    group_size = channels // groups
    chunk = feature_taps.shape[2]

    row = jnp.concatenate([filters.reshape(-1), feature_taps.reshape(-1), skip_gain])
    gathered = lax.all_to_all(
        jnp.broadcast_to(row[None], (ctx_size, row.shape[0])), "ctx", 0, 0, tiled=True
    )
    n_filt = groups * taps_here
    n_chunk = row.shape[0] - n_filt
    per_block = ctx_size // fsdp_size
    filters_all = (
        gathered[:, :n_filt]
        .reshape(ctx_size, groups, taps_here)
        .transpose(1, 0, 2)
        .reshape(groups, taps_count)
    )
    moved = lax.all_to_all(gathered[:, n_filt:], "fsdp", 0, 0, tiled=True)
    local = (
        moved.reshape(fsdp_size, per_block, n_chunk).transpose(1, 0, 2).reshape(ctx_size, n_chunk)
    )
    taps_all = (
        local[:, : 9 * chunk].reshape(ctx_size, 3, 3, chunk).transpose(1, 2, 0, 3).reshape(3, 3, channels)
    )
    skip_all = local[:, 9 * chunk :].reshape(channels)

    rim = reach_cols + 2
    prev_rim = passed_along(
        jnp.concatenate(
            [outer_gate[:, block_len - 2 :], inner_gate[:, block_len - rim :], value_stream[:, block_len - rim :]],
            axis=1,
        ),
        "ctx",
        1,
    )
    next_rim = passed_along(
        jnp.concatenate(
            [grad_output[:, :rim], outer_gate[:, :rim], inner_gate[:, :2], value_stream[:, :2]], axis=1
        ),
        "ctx",
        -1,
    )
    outer_ext = jnp.concatenate([prev_rim[:, :2], outer_gate, next_rim[:, rim : 2 * rim]], axis=1)
    inner_ext = jnp.concatenate(
        [prev_rim[:, 2 : 2 + rim], inner_gate, next_rim[:, 2 * rim : 2 * rim + 2]], axis=1
    )
    value_ext = jnp.concatenate([prev_rim[:, 2 + rim :], value_stream, next_rim[:, 2 * rim + 2 :]], axis=1)
    upstream = jnp.concatenate([grad_output, next_rim[:, :rim]], axis=1).astype(jnp.float32)

    outer_feat = featurize(outer_ext.astype(jnp.float32), taps_all[0])
    inner_feat = featurize(inner_ext.astype(jnp.float32), taps_all[1])
    value_feat = featurize(value_ext.astype(jnp.float32), taps_all[2])
    product = (inner_feat * value_feat).astype(jnp.bfloat16)

    out_len = block_len + 2
    filters_low = filters_all.astype(jnp.bfloat16)
    product_here = product[:, reach_cols:].astype(jnp.float32)
    grad_mixed = (upstream * outer_feat).astype(jnp.bfloat16)
    convolved, ahead, filter_diag = both_convs(product, grad_mixed, filters_low, block_len)
    mixed = convolved + skip_all[:, None] * product_here

    grad_outer_feat = (upstream[:, :out_len] * mixed).astype(jnp.bfloat16)
    grad_product = ahead + skip_all[:, None] * grad_mixed[:, :out_len].astype(jnp.float32)
    grad_inner_feat = (grad_product * value_feat[:, reach_cols:]).astype(jnp.bfloat16)
    grad_value_feat = (grad_product * inner_feat[:, reach_cols:]).astype(jnp.bfloat16)

    grad_scale = 1.0 / math.sqrt(ctx_size * block_len)
    gm_here = grad_mixed[:, :block_len]
    filter_part = grad_scale * filter_diag[:, ::-1]
    skip_part = grad_scale * jnp.sum(
        gm_here.astype(jnp.float32) * product_here[:, :block_len], axis=1
    )
    taps_part = grad_scale * jnp.stack(
        [
            tap_sums(grad_outer_feat[:, :block_len], outer_ext[:, : block_len + 2]),
            tap_sums(grad_inner_feat[:, :block_len], inner_ext[:, reach_cols : reach_cols + block_len + 2]),
            tap_sums(grad_value_feat[:, :block_len], value_ext[:, reach_cols : reach_cols + block_len + 2]),
        ]
    )

    chunk_parts = jnp.concatenate(
        [
            taps_part.reshape(3, 3, ctx_size, chunk).transpose(2, 0, 1, 3).reshape(ctx_size, -1),
            skip_part.reshape(ctx_size, chunk),
        ],
        axis=1,
    )
    to_fsdp = chunk_parts.reshape(per_block, fsdp_size, n_chunk).transpose(1, 0, 2).reshape(ctx_size, n_chunk)
    to_fsdp, outer_feat, mixed, grad_outer_feat = lax.optimization_barrier(
        (to_fsdp, outer_feat, mixed, grad_outer_feat)
    )
    by_owner = lax.all_to_all(to_fsdp, "fsdp", 0, 0, tiled=True)
    gated_out = (outer_feat[:, :block_len] * mixed[:, :block_len]).astype(jnp.bfloat16)
    grad_outer = carry_back(grad_outer_feat.astype(jnp.float32), taps_all[0])
    by_owner, grad_inner_feat, grad_value_feat = lax.optimization_barrier(
        (by_owner, grad_inner_feat, grad_value_feat)
    )
    grad_inner = carry_back(grad_inner_feat.astype(jnp.float32), taps_all[1])
    grad_value = carry_back(grad_value_feat.astype(jnp.float32), taps_all[2])

    send = jnp.concatenate(
        [
            filter_part.reshape(groups, ctx_size, taps_here).transpose(1, 0, 2).reshape(ctx_size, -1),
            by_owner,
        ],
        axis=1,
    )
    reduced = jnp.sum(lax.all_to_all(send, "ctx", 0, 0, tiled=True), axis=0)
    filter_share = reduced[:n_filt].reshape(groups, taps_here)
    taps_share = reduced[n_filt : n_filt + 9 * chunk].reshape(3, 3, chunk)
    skip_share = reduced[n_filt + 9 * chunk :]
    return (
        gated_out,
        grad_outer.astype(jnp.bfloat16),
        grad_inner.astype(jnp.bfloat16),
        grad_value.astype(jnp.bfloat16),
        filter_share,
        taps_share,
        skip_share,
    )


def solution(mesh):
    return jax.shard_map(
        shards,
        mesh=mesh,
        in_specs=(
            P("fsdp", "ctx"),
            P("fsdp", "ctx"),
            P("fsdp", "ctx"),
            P("fsdp", "ctx"),
            P("fsdp", "ctx"),
            P(None, None, ("ctx", "fsdp")),
            P(("ctx", "fsdp")),
        ),
        out_specs=(
            P("fsdp", "ctx"),
            P("fsdp", "ctx"),
            P("fsdp", "ctx"),
            P("fsdp", "ctx"),
            P("fsdp", "ctx"),
            P(None, None, ("ctx", "fsdp")),
            P(("ctx", "fsdp")),
        ),
        check_vma=False,
    )
```
